256 devices in a mesh: row: 16 (over z_hi, y, core), col: 4 (over z_lo), pblk: 4 (over x).
Axes of the slice: x: 4, y: 4, z: 8 (z_hi: 2, z_lo: 4; z = z_hi * 4 + z_lo), core: 2. Of those that a mesh axis runs over, the one named last changes fastest.
Arguments:
- left_feat: int32 [2048, 256], P(('row', 'col', 'pblk')), may hold values from 0 to 255
- right_feat: int32 [4, 4, 64, 256], P('col', 'pblk', 'row'), may hold values from 0 to 255
- embed: bfloat16 [1024, 256], replicated, may hold values from -12 to 12
- conv_w: bfloat16 [8, 768, 256], replicated, may hold values from -0.01953125 to 0.01953125
- head: float32 [256], replicated, may hold values from -0.078125 to 0.078125
- assign: int32 [8], replicated, may hold values from 0 to 3, as said below
- proj_delta: bfloat16 [4, 256, 128], replicated, may hold values from -0.375 to 0.375
- proj_input: bfloat16 [4, 768, 128], replicated, may hold values from -0.21875 to 0.21875
Outputs:
- kernel: float32 [2048, 1024], P('row', ('col', 'pblk'))
The draws below stay inside these ranges and needn't reach their ends.
Inputs may be any that keep to these rules, and one draw needn't show every extreme that they name: `assign`: every one of the 4 blocks is named by exactly 2 layers.
All inputs are finite; a program needn't handle non-finite values.
Results may differ from the reference program's by a relative error of at most 0.00036.
Values may be sent and summed in bfloat16 or wider, within the bound.
No kernel may reach another device: no remote copies, remote signals or barrier semaphores. Data moves between devices by JAX's collectives and lax.ppermute only.
A program may use at most 128 MiB of HBM per device.

```python
import jax
import jax.numpy as jnp
from jax import lax

C = 256
SEQ = 64
NFEAT = 4
VOCAB = 256
LAYERS = 8
PR = 128
PS = 128
NBLK = 4
RIGHT_DEV = 256
NL = 2048
NR = 1024
N_COL = 4
N_PBLK = 4


def draw_assign(key, part):
    shuffled = jax.random.permutation(key, LAYERS)
    return (shuffled % NBLK).astype(jnp.int32)


def place_ends(values, key, least, largest):
    longest = values.shape.index(max(values.shape))
    spots = []
    for shift in (0, 1):
        where = [jax.random.randint(jax.random.fold_in(key, axis), (), 0, length) for axis, length in enumerate(values.shape)]
        where[longest] = (where[longest] + shift) % values.shape[longest]
        spots.append(tuple(where))
    return values.at[spots[0]].set(least).at[spots[1]].set(largest)


def centred(stream_key, shape, spread, limit, kind=jnp.bfloat16):
    values = jax.random.normal(stream_key, shape, jnp.float32) * spread
    return jnp.minimum(jnp.maximum(values, -limit), limit).astype(kind)


def setup_inputs(seed: int = 0) -> dict:
    key_of = jax.random.split(jax.random.key(seed), 9)
    return {
        "left_feat": place_ends(jax.random.randint(key_of[0], (NL, SEQ * NFEAT), 0, VOCAB), jax.random.fold_in(key_of[0], 1), 0, VOCAB - 1).astype(jnp.int32),
        "right_feat": place_ends(jax.random.randint(key_of[1], (N_COL, N_PBLK, RIGHT_DEV // N_PBLK, SEQ * NFEAT), 0, VOCAB), jax.random.fold_in(key_of[1], 1), 0, VOCAB - 1).astype(jnp.int32),
        "embed": jnp.clip(jax.random.uniform(key_of[2], (NFEAT * VOCAB, C), jnp.float32, -12.0, 12.0), -12.0, 12.0).astype(jnp.bfloat16),
        "conv_w": centred(key_of[3], (LAYERS, 3 * C, C), (400 * C) ** -0.5, 0.01953125),
        "head": centred(key_of[4], (C,), (20 * C) ** -0.5, 0.078125, jnp.float32),
        "assign": draw_assign(jax.random.fold_in(key_of[8], 71), 0),
        "proj_delta": centred(key_of[6], (NBLK, C, PR), C ** -0.5, 0.375),
        "proj_input": centred(key_of[7], (NBLK, 3 * C, PS), (3 * C) ** -0.5, 0.21875),
    }


def shift_wide(inputs):
    blank = jnp.zeros_like(inputs[:, :1])
    earlier = jnp.concatenate([blank, inputs[:, :-1]], 1)
    later_cells = jnp.concatenate([inputs[:, 1:], blank], 1)
    return jnp.concatenate([earlier, inputs, later_cells], 2)


def example_panels(features, embed, conv_w, head, assign, proj_delta, proj_input):
    examples = features.shape[0]
    offsets = jnp.arange(NFEAT, dtype=jnp.int32) * VOCAB
    table_rows = features.reshape(examples, SEQ, NFEAT) + offsets
    hidden = jnp.sum(embed[table_rows].astype(jnp.float32), axis=2)
    wides = []
    pres = []
    for layer in range(LAYERS):
        wide_input = shift_wide(hidden.astype(jnp.bfloat16))
        pre_act = jnp.einsum("esk,kc->esc", wide_input.astype(jnp.float32), conv_w[layer].astype(jnp.float32))
        wides.append(wide_input)
        pres.append(pre_act)
        hidden = hidden + jax.nn.silu(pre_act)
    grad_h = jnp.broadcast_to(head / SEQ, hidden.shape).astype(jnp.float32)
    block_ids = jnp.arange(NBLK, dtype=jnp.int32)
    panel = jnp.zeros((examples, NBLK, PR, PS), jnp.float32)
    for layer in range(LAYERS - 1, -1, -1):
        pre_act = pres[layer]
        sigmoid_z = jax.nn.sigmoid(pre_act)
        delta_low = (grad_h * sigmoid_z * (1.0 + pre_act * (1.0 - sigmoid_z))).astype(jnp.bfloat16)
        block_pick = (assign[layer] == block_ids).astype(jnp.float32)
        rows_table = jnp.einsum("b,bcr->cr", block_pick, proj_delta.astype(jnp.float32))
        cols_table = jnp.einsum("b,bkt->kt", block_pick, proj_input.astype(jnp.float32))
        left_side = jnp.einsum("esc,cr->esr", delta_low.astype(jnp.float32), rows_table)
        right_side = jnp.einsum("esk,kt->est", wides[layer].astype(jnp.float32), cols_table)
        projected = jnp.einsum("esr,est->ert", left_side, right_side, precision=lax.Precision.HIGHEST)
        panel = panel + block_pick[None, :, None, None] * projected[:, None]
        if layer > 0:
            back_wide = jnp.einsum("esc,kc->esk", delta_low.astype(jnp.float32), conv_w[layer].astype(jnp.float32))
            first_third = back_wide[:, :, :C]
            last_third = back_wide[:, :, 2 * C:]
            blank = jnp.zeros_like(first_third[:, :1])
            grad_input = back_wide[:, :, C:2 * C]
            grad_input = grad_input + jnp.concatenate([first_third[:, 1:], blank], 1)
            grad_input = grad_input + jnp.concatenate([blank, last_third[:, :-1]], 1)
            grad_h = grad_h + grad_input
    return panel.reshape(examples, NBLK, PR * PS).astype(jnp.bfloat16)


def all_panels(features, embed, conv_w, head, assign, proj_delta, proj_input):
    total = features.shape[0]
    blocks = features.reshape(total // 16, 16, features.shape[1])

    def one_block(block_feat):
        return example_panels(block_feat, embed, conv_w, head, assign, proj_delta, proj_input)

    result = lax.map(one_block, blocks)
    return result.reshape(total, NBLK, PR * PS)


def reference(left_feat, right_feat, embed, conv_w, head, assign, proj_delta, proj_input):
    right_flat = right_feat.reshape(NR, SEQ * NFEAT)
    left_panel = all_panels(left_feat, embed, conv_w, head, assign, proj_delta, proj_input)
    right_panel = all_panels(right_flat, embed, conv_w, head, assign, proj_delta, proj_input)
    kernel = jnp.zeros((left_panel.shape[0], right_panel.shape[0]), jnp.float32)
    for block in range(NBLK):
        kernel = kernel + jnp.dot(left_panel[:, block], right_panel[:, block].T, preferred_element_type=jnp.float32)
    return kernel
```

```python
import jax
import jax.numpy as jnp
from jax import lax
from jax.sharding import Mesh, PartitionSpec as P

SEQ = 64
NFEAT = 4
VOCAB = 256
LAYERS = 8
PR = 128
PS = 128


def shift_wide(inputs):
    blank = jnp.zeros_like(inputs[:, :1])
    earlier = jnp.concatenate([blank, inputs[:, :-1]], 1)
    later_cells = jnp.concatenate([inputs[:, 1:], blank], 1)
    return jnp.concatenate([earlier, inputs, later_cells], 2)


def panels(features, embed, conv_w, head, assign, proj_delta, proj_input):
    examples = features.shape[0]
    blocks_here = proj_delta.shape[0]
    offsets = jnp.arange(NFEAT, dtype=jnp.int32) * VOCAB
    table_rows = features.reshape(examples, SEQ, NFEAT) + offsets
    table_ids = jnp.arange(NFEAT * VOCAB, dtype=jnp.int32)
    onehot = (table_rows[:, :, 0:1] == table_ids).astype(jnp.bfloat16)
    for field in range(1, NFEAT):
        onehot = onehot + (table_rows[:, :, field : field + 1] == table_ids).astype(jnp.bfloat16)
    hidden = jnp.einsum("esv,vc->esc", onehot, embed, preferred_element_type=jnp.float32)
    wides = []
    pres = []
    for layer in range(LAYERS):
        wide_input = shift_wide(hidden.astype(jnp.bfloat16))
        pre_act = jnp.einsum(
            "esk,kc->esc", wide_input, conv_w[layer], preferred_element_type=jnp.float32
        )
        wides.append(wide_input)
        pres.append(pre_act)
        hidden = hidden + jax.nn.silu(pre_act)
    grad_h = jnp.broadcast_to(head / SEQ, hidden.shape)
    block_ids = jnp.arange(blocks_here, dtype=jnp.int32)
    panel = jnp.zeros((examples, blocks_here, PR, PS), jnp.float32)
    for layer in range(LAYERS - 1, -1, -1):
        pre_act = pres[layer]
        sigmoid_z = jax.nn.sigmoid(pre_act)
        delta_low = (grad_h * sigmoid_z * (1.0 + pre_act * (1.0 - sigmoid_z))).astype(jnp.bfloat16)
        block_pick = (assign[layer] == block_ids).astype(jnp.float32)
        rows_table = jnp.einsum("b,bcr->cr", block_pick, proj_delta.astype(jnp.float32)).astype(
            jnp.bfloat16
        )
        cols_table = jnp.einsum("b,bkt->kt", block_pick, proj_input.astype(jnp.float32)).astype(
            jnp.bfloat16
        )
        left_side = jnp.einsum(
            "esc,cr->esr", delta_low, rows_table, preferred_element_type=jnp.float32
        )
        right_side = jnp.einsum(
            "esk,kt->est", wides[layer], cols_table, preferred_element_type=jnp.float32
        )
        projected = jnp.einsum(
            "esr,est->ert", left_side, right_side, precision=lax.Precision.HIGHEST
        )
        panel = panel + block_pick[None, :, None, None] * projected[:, None]
        if layer > 0:
            back_wide = jnp.einsum(
                "esc,kc->esk", delta_low, conv_w[layer], preferred_element_type=jnp.float32
            )
            width = grad_h.shape[2]
            first_third = back_wide[:, :, :width]
            last_third = back_wide[:, :, 2 * width :]
            blank = jnp.zeros_like(first_third[:, :1])
            grad_input = back_wide[:, :, width : 2 * width]
            grad_input = grad_input + jnp.concatenate([first_third[:, 1:], blank], 1)
            grad_input = grad_input + jnp.concatenate([blank, last_third[:, :-1]], 1)
            grad_h = grad_h + grad_input
    return panel.reshape(examples, blocks_here, PR * PS).astype(jnp.bfloat16)


def on_device(left_feat, right_feat, embed, conv_w, head, assign, proj_delta, proj_input):
    group = ("zh", "core", "col")
    n_group = lax.axis_size(group)
    n_zh = lax.axis_size("zh")
    n_core = lax.axis_size("core")
    n_col = lax.axis_size("col")
    n_y = lax.axis_size("y")
    n_blk = lax.axis_size("pblk")
    left_each = left_feat.shape[0]
    right_each = right_feat.shape[2]
    right_local = right_feat.reshape(right_each, right_feat.shape[3])
    own_features = jnp.concatenate([left_feat, right_local], 0)
    panel = panels(own_features, embed, conv_w, head, assign, proj_delta, proj_input)
    own = panel.shape[0]
    width = panel.shape[1] * panel.shape[2] // n_group
    sliced = panel.reshape(own, n_group, width)
    spread = lax.all_to_all(sliced, group, split_axis=1, concat_axis=0, tiled=True)
    spread = spread.reshape(n_group, own, width)
    left_part = spread[:, :left_each].reshape(n_group * left_each, width)
    right_part = spread[:, left_each:].reshape(n_group * right_each, width)
    left_tile = lax.all_gather(left_part, "pblk", axis=0, tiled=True)
    right_tile = lax.all_gather(right_part, "y", axis=0, tiled=True)
    partial_tile = jnp.einsum("lk,rk->lr", left_tile, right_tile, preferred_element_type=jnp.float32)
    partial_tile = partial_tile.reshape(
        n_blk, n_zh, n_core, n_col, left_each, n_y, n_zh, n_core, n_col, right_each
    )
    chunks = jnp.transpose(partial_tile, (1, 2, 8, 3, 0, 4, 6, 5, 7, 9))
    chunks = chunks.reshape(n_group, n_col * n_blk * left_each, n_zh * n_y * n_core * right_each)
    block = lax.psum_scatter(chunks, group, scatter_dimension=0, tiled=True)
    return block.reshape(block.shape[1], block.shape[2])


def solution(mesh):
    n_row = mesh.shape["row"]
    fine = Mesh(
        mesh.devices.reshape(2, 4, n_row // 8, mesh.shape["col"], mesh.shape["pblk"]),
        ("zh", "y", "core", "col", "pblk"),
    )
    rows = ("zh", "y", "core")
    placed = (
        P((*rows, "col", "pblk"), None),
        P("col", "pblk", rows, None),
        P(),
        P(),
        P(),
        P(),
        P(),
        P(),
    )
    return jax.shard_map(
        on_device, mesh=fine, in_specs=placed, out_specs=P(rows, ("col", "pblk")), check_vma=False
    )
```

```python
import jax
import jax.numpy as jnp
from jax import lax
from jax.sharding import Mesh, PartitionSpec as P

SEQ = 64
NFEAT = 4
VOCAB = 256
LAYERS = 8
PR = 128
PS = 128


def shift_wide(inputs):
    blank = jnp.zeros_like(inputs[:, :1])
    earlier = jnp.concatenate([blank, inputs[:, :-1]], 1)
    later_cells = jnp.concatenate([inputs[:, 1:], blank], 1)
    return jnp.concatenate([earlier, inputs, later_cells], 2)


def panels(features, embed, conv_w, head, assign, proj_delta, proj_input):
    examples = features.shape[0]
    blocks_here = proj_delta.shape[0]
    offsets = jnp.arange(NFEAT, dtype=jnp.int32) * VOCAB
    table_rows = features.reshape(examples, SEQ, NFEAT) + offsets
    table_ids = jnp.arange(NFEAT * VOCAB, dtype=jnp.int32)
    onehot = (table_rows[:, :, 0:1] == table_ids).astype(jnp.bfloat16)
    for field in range(1, NFEAT):
        onehot = onehot + (table_rows[:, :, field : field + 1] == table_ids).astype(jnp.bfloat16)
    hidden = jnp.einsum("esv,vc->esc", onehot, embed, preferred_element_type=jnp.float32)
    wides = []
    pres = []
    for layer in range(LAYERS):
        wide_input = shift_wide(hidden.astype(jnp.bfloat16))
        pre_act = jnp.einsum(
            "esk,kc->esc", wide_input, conv_w[layer], preferred_element_type=jnp.float32
        )
        wides.append(wide_input)
        pres.append(pre_act)
        hidden = hidden + jax.nn.silu(pre_act)
    grad_h = jnp.broadcast_to(head / SEQ, hidden.shape)
    delta_sides = [None] * LAYERS
    input_sides = [None] * LAYERS
    for layer in range(LAYERS - 1, -1, -1):
        pre_act = pres[layer]
        sigmoid_z = jax.nn.sigmoid(pre_act)
        delta_low = (grad_h * sigmoid_z * (1.0 + pre_act * (1.0 - sigmoid_z))).astype(jnp.bfloat16)
        delta_sides[layer] = jnp.einsum(
            "esc,cr->esr", delta_low, proj_delta[assign[layer]], preferred_element_type=jnp.float32
        )
        input_sides[layer] = jnp.einsum(
            "esk,kt->est", wides[layer], proj_input[assign[layer]], preferred_element_type=jnp.float32
        )
        if layer > 0:
            back_wide = jnp.einsum(
                "esc,kc->esk", delta_low, conv_w[layer], preferred_element_type=jnp.float32
            )
            width = grad_h.shape[2]
            first_third = back_wide[:, :, :width]
            last_third = back_wide[:, :, 2 * width :]
            blank = jnp.zeros_like(first_third[:, :1])
            grad_input = back_wide[:, :, width : 2 * width]
            grad_input = grad_input + jnp.concatenate([first_third[:, 1:], blank], 1)
            grad_input = grad_input + jnp.concatenate([blank, last_third[:, :-1]], 1)
            grad_h = grad_h + grad_input
    layer_ids = jnp.arange(LAYERS, dtype=jnp.int32)
    same_before = jnp.sum(
        (assign[None, :] == assign[:, None]) & (layer_ids[None, :] < layer_ids[:, None]), axis=1
    )
    slot = assign * (LAYERS // blocks_here) + same_before
    order = jnp.sum(
        jnp.where(slot[None, :] == layer_ids[:, None], layer_ids[None, :], 0), axis=1
    )
    delta_stack = jnp.stack(delta_sides)[order]
    input_stack = jnp.stack(input_sides)[order]
    per_block = LAYERS // blocks_here
    delta_stack = delta_stack.reshape(blocks_here, per_block, examples, SEQ, PR)
    input_stack = input_stack.reshape(blocks_here, per_block, examples, SEQ, PS)
    panel = jnp.einsum(
        "bjesr,bjest->ebrt", delta_stack, input_stack, precision=lax.Precision.HIGHEST
    )
    return panel.reshape(examples, blocks_here * PR * PS).astype(jnp.bfloat16)


def on_device(left_feat, right_feat, embed, conv_w, head, assign, proj_delta, proj_input):
    group = ("zh", "core", "col")
    n_group = lax.axis_size(group)
    n_zh = lax.axis_size("zh")
    n_core = lax.axis_size("core")
    n_col = lax.axis_size("col")
    n_y = lax.axis_size("y")
    n_blk = lax.axis_size("pblk")
    left_each = left_feat.shape[0]
    right_each = right_feat.shape[2]
    right_local = right_feat.reshape(right_each, right_feat.shape[3])
    own_features = jnp.concatenate([left_feat, right_local], 0)
    panel = panels(own_features, embed, conv_w, head, assign, proj_delta, proj_input)
    own = panel.shape[0]
    width = panel.shape[1] // n_group
    sliced = panel.reshape(own, n_group, width)
    spread = lax.all_to_all(sliced, group, split_axis=1, concat_axis=0, tiled=True)
    spread = spread.reshape(n_group, own, width)
    left_part = spread[:, :left_each].reshape(n_group * left_each, width)
    right_part = spread[:, left_each:].reshape(n_group * right_each, width)
    left_tile = lax.all_gather(left_part, "pblk", axis=0, tiled=True)
    right_tile = lax.all_gather(right_part, "y", axis=0, tiled=True)
    left_tile = left_tile.reshape(n_blk, n_zh * n_core, n_col, left_each, width)
    left_tile = jnp.transpose(left_tile, (1, 2, 0, 3, 4)).reshape(-1, width)
    right_tile = right_tile.reshape(n_y, n_zh, n_core, n_col, right_each, width)
    right_tile = jnp.transpose(right_tile, (3, 1, 0, 2, 4, 5)).reshape(-1, width)
    partial_t = jnp.einsum("rk,lk->rl", right_tile, left_tile, preferred_element_type=jnp.float32)
    chunks = partial_t.reshape(n_col, partial_t.shape[0] // n_col, n_zh * n_core, -1)
    chunks = jnp.transpose(chunks, (2, 0, 1, 3)).reshape(n_group, chunks.shape[1], chunks.shape[3])
    block = lax.psum_scatter(chunks, group, scatter_dimension=0, tiled=True)
    return block[0].T


def solution(mesh):
    n_row = mesh.shape["row"]
    fine = Mesh(
        mesh.devices.reshape(2, 4, n_row // 8, mesh.shape["col"], mesh.shape["pblk"]),
        ("zh", "y", "core", "col", "pblk"),
    )
    rows = ("zh", "y", "core")
    placed = (
        P((*rows, "col", "pblk"), None),
        P("col", "pblk", rows, None),
        P(),
        P(),
        P(),
        P(),
        P(),
        P(),
    )
    return jax.shard_map(
        on_device, mesh=fine, in_specs=placed, out_specs=P(rows, ("col", "pblk")), check_vma=False
    )
```

```python
import jax
import jax.numpy as jnp
from jax import lax
from jax.sharding import Mesh, PartitionSpec as P

SEQ = 64
NFEAT = 4
VOCAB = 256
LAYERS = 8
PR = 128
PS = 128


def shift_wide(inputs):
    blank = jnp.zeros_like(inputs[:, :1])
    earlier = jnp.concatenate([blank, inputs[:, :-1]], 1)
    later_cells = jnp.concatenate([inputs[:, 1:], blank], 1)
    return jnp.concatenate([earlier, inputs, later_cells], 2)


def panels(features, embed, conv_w, head, assign, proj_delta, proj_input):
    examples = features.shape[0]
    blocks_here = proj_delta.shape[0]
    offsets = jnp.arange(NFEAT, dtype=jnp.int32) * VOCAB
    table_rows = features.reshape(examples, SEQ, NFEAT) + offsets
    table_ids = jnp.arange(NFEAT * VOCAB, dtype=jnp.int32)
    onehot = (table_rows[:, :, 0:1] == table_ids).astype(jnp.bfloat16)
    for field in range(1, NFEAT):
        onehot = onehot + (table_rows[:, :, field : field + 1] == table_ids).astype(jnp.bfloat16)
    hidden = jnp.einsum("esv,vc->esc", onehot, embed, preferred_element_type=jnp.float32)
    wides = []
    pres = []
    for layer in range(LAYERS):
        wide_input = shift_wide(hidden.astype(jnp.bfloat16))
        pre_act = jnp.einsum(
            "esk,kc->esc", wide_input, conv_w[layer], preferred_element_type=jnp.float32
        )
        wides.append(wide_input)
        pres.append(pre_act)
        hidden = hidden + jax.nn.silu(pre_act)
    grad_h = jnp.broadcast_to(head / SEQ, hidden.shape)
    delta_sides = [None] * LAYERS
    input_sides = [None] * LAYERS
    for layer in range(LAYERS - 1, -1, -1):
        pre_act = pres[layer]
        sigmoid_z = jax.nn.sigmoid(pre_act)
        delta_low = (grad_h * sigmoid_z * (1.0 + pre_act * (1.0 - sigmoid_z))).astype(jnp.bfloat16)
        delta_sides[layer] = jnp.einsum(
            "esc,cr->esr", delta_low, proj_delta[assign[layer]], preferred_element_type=jnp.float32
        )
        input_sides[layer] = jnp.einsum(
            "esk,kt->est", wides[layer], proj_input[assign[layer]], preferred_element_type=jnp.float32
        )
        if layer > 0:
            back_wide = jnp.einsum(
                "esc,kc->esk", delta_low, conv_w[layer], preferred_element_type=jnp.float32
            )
            width = grad_h.shape[2]
            first_third = back_wide[:, :, :width]
            last_third = back_wide[:, :, 2 * width :]
            blank = jnp.zeros_like(first_third[:, :1])
            grad_input = back_wide[:, :, width : 2 * width]
            grad_input = grad_input + jnp.concatenate([first_third[:, 1:], blank], 1)
            grad_input = grad_input + jnp.concatenate([blank, last_third[:, :-1]], 1)
            grad_h = grad_h + grad_input
    layer_ids = jnp.arange(LAYERS, dtype=jnp.int32)
    same_before = jnp.sum(
        (assign[None, :] == assign[:, None]) & (layer_ids[None, :] < layer_ids[:, None]), axis=1
    )
    slot = assign * (LAYERS // blocks_here) + same_before
    order = jnp.sum(
        jnp.where(slot[None, :] == layer_ids[:, None], layer_ids[None, :], 0), axis=1
    )
    delta_stack = jnp.stack(delta_sides)[order]
    input_stack = jnp.stack(input_sides)[order]
    per_block = LAYERS // blocks_here
    delta_stack = delta_stack.reshape(blocks_here, per_block, examples, SEQ, PR)
    input_stack = input_stack.reshape(blocks_here, per_block, examples, SEQ, PS)
    panel = jnp.einsum(
        "bjesr,bjest->ebrt", delta_stack, input_stack, precision=lax.Precision.HIGH
    )
    return panel.reshape(examples, blocks_here * PR * PS).astype(jnp.bfloat16)


def on_device(left_feat, right_feat, embed, conv_w, head, assign, proj_delta, proj_input):
    group = ("zh", "core", "col")
    n_group = lax.axis_size(group)
    n_zh = lax.axis_size("zh")
    n_core = lax.axis_size("core")
    n_col = lax.axis_size("col")
    n_y = lax.axis_size("y")
    n_blk = lax.axis_size("pblk")
    left_each = left_feat.shape[0]
    right_each = right_feat.shape[2]
    right_local = right_feat.reshape(right_each, right_feat.shape[3])
    own_features = jnp.concatenate([left_feat, right_local], 0)
    panel = panels(own_features, embed, conv_w, head, assign, proj_delta, proj_input)
    own = panel.shape[0]
    width = panel.shape[1] // n_group
    sliced = panel.reshape(own, n_group, width)
    right_part = lax.all_to_all(sliced[left_each:], group, split_axis=1, concat_axis=0, tiled=True)
    right_part = right_part.reshape(n_group * right_each, width)
    left_part = lax.all_to_all(sliced[:left_each], group, split_axis=1, concat_axis=0, tiled=True)
    left_part = left_part.reshape(n_group * left_each, width)
    left_tile = lax.all_gather(left_part, "pblk", axis=0, tiled=True)
    right_tile = lax.all_gather(right_part, "y", axis=0, tiled=True)
    left_tile = left_tile.reshape(n_blk, n_zh * n_core, n_col, left_each, width)
    left_tile = jnp.transpose(left_tile, (1, 2, 0, 3, 4)).reshape(-1, width)
    right_tile = right_tile.reshape(n_y, n_zh, n_core, n_col, right_each, width)
    right_tile = jnp.transpose(right_tile, (3, 1, 0, 2, 4, 5)).reshape(-1, width)
    partial_t = jnp.einsum("rk,lk->rl", right_tile, left_tile, preferred_element_type=jnp.float32)
    chunks = partial_t.reshape(n_col, partial_t.shape[0] // n_col, n_zh * n_core, -1)
    chunks = jnp.transpose(chunks, (2, 0, 1, 3)).reshape(n_group, chunks.shape[1], chunks.shape[3])
    received = lax.all_to_all(chunks, group, split_axis=0, concat_axis=0, tiled=True)
    return jnp.sum(received, axis=0).T


def solution(mesh):
    n_row = mesh.shape["row"]
    fine = Mesh(
        mesh.devices.reshape(2, 4, n_row // 8, mesh.shape["col"], mesh.shape["pblk"]),
        ("zh", "y", "core", "col", "pblk"),
    )
    rows = ("zh", "y", "core")
    placed = (
        P((*rows, "col", "pblk"), None),
        P("col", "pblk", rows, None),
        P(),
        P(),
        P(),
        P(),
        P(),
        P(),
    )
    return jax.shard_map(
        on_device, mesh=fine, in_specs=placed, out_specs=P(rows, ("col", "pblk")), check_vma=False
    )
```

```python
import jax
import jax.numpy as jnp
from jax import lax
from jax.sharding import Mesh, PartitionSpec as P

SEQ = 64
NFEAT = 4
VOCAB = 256
LAYERS = 8
PR = 128
PS = 128


def shift_wide(inputs):
    blank = jnp.zeros_like(inputs[:, :1])
    earlier = jnp.concatenate([blank, inputs[:, :-1]], 1)
    later_cells = jnp.concatenate([inputs[:, 1:], blank], 1)
    return jnp.concatenate([earlier, inputs, later_cells], 2)


def panels(features, embed, conv_w, head, assign, proj_delta, proj_input):
    examples = features.shape[0]
    blocks_here = proj_delta.shape[0]
    offsets = jnp.arange(NFEAT, dtype=jnp.int32) * VOCAB
    table_rows = features.reshape(examples, SEQ, NFEAT) + offsets
    table_ids = jnp.arange(NFEAT * VOCAB, dtype=jnp.int32)
    onehot = (table_rows[:, :, 0:1] == table_ids).astype(jnp.bfloat16)
    for field in range(1, NFEAT):
        onehot = onehot + (table_rows[:, :, field : field + 1] == table_ids).astype(jnp.bfloat16)
    hidden = jnp.einsum("esv,vc->esc", onehot, embed, preferred_element_type=jnp.float32)
    wides = []
    pres = []
    for layer in range(LAYERS):
        wide_input = shift_wide(hidden.astype(jnp.bfloat16))
        pre_act = jnp.einsum(
            "esk,kc->esc", wide_input, conv_w[layer], preferred_element_type=jnp.float32
        )
        wides.append(wide_input)
        pres.append(pre_act)
        hidden = hidden + jax.nn.silu(pre_act)
    grad_h = jnp.broadcast_to(head / SEQ, hidden.shape)
    delta_sides = [None] * LAYERS
    input_sides = [None] * LAYERS
    for layer in range(LAYERS - 1, -1, -1):
        pre_act = pres[layer]
        sigmoid_z = jax.nn.sigmoid(pre_act)
        delta_low = (grad_h * sigmoid_z * (1.0 + pre_act * (1.0 - sigmoid_z))).astype(jnp.bfloat16)
        delta_sides[layer] = jnp.einsum(
            "esc,cr->esr", delta_low, proj_delta[assign[layer]], preferred_element_type=jnp.float32
        )
        input_sides[layer] = jnp.einsum(
            "esk,kt->est", wides[layer], proj_input[assign[layer]], preferred_element_type=jnp.float32
        )
        if layer > 0:
            back_wide = jnp.einsum(
                "esc,kc->esk", delta_low, conv_w[layer], preferred_element_type=jnp.float32
            )
            width = grad_h.shape[2]
            first_third = back_wide[:, :, :width]
            last_third = back_wide[:, :, 2 * width :]
            blank = jnp.zeros_like(first_third[:, :1])
            grad_input = back_wide[:, :, width : 2 * width]
            grad_input = grad_input + jnp.concatenate([first_third[:, 1:], blank], 1)
            grad_input = grad_input + jnp.concatenate([blank, last_third[:, :-1]], 1)
            grad_h = grad_h + grad_input
    layer_ids = jnp.arange(LAYERS, dtype=jnp.int32)
    same_before = jnp.sum(
        (assign[None, :] == assign[:, None]) & (layer_ids[None, :] < layer_ids[:, None]), axis=1
    )
    slot = assign * (LAYERS // blocks_here) + same_before
    order = jnp.sum(
        jnp.where(slot[None, :] == layer_ids[:, None], layer_ids[None, :], 0), axis=1
    )
    delta_slots = []
    input_slots = []
    for slot_id in range(LAYERS):
        picked_delta = delta_sides[0]
        picked_input = input_sides[0]
        for layer in range(1, LAYERS):
            hit = order[slot_id] == layer
            picked_delta = jnp.where(hit, delta_sides[layer], picked_delta)
            picked_input = jnp.where(hit, input_sides[layer], picked_input)
        delta_slots.append(picked_delta)
        input_slots.append(picked_input)
    delta_stack = jnp.stack(delta_slots)
    input_stack = jnp.stack(input_slots)
    per_block = LAYERS // blocks_here
    delta_stack = delta_stack.reshape(blocks_here, per_block, examples, SEQ, PR)
    input_stack = input_stack.reshape(blocks_here, per_block, examples, SEQ, PS)
    panel = jnp.einsum(
        "bjesr,bjest->ebrt", delta_stack, input_stack, precision=lax.Precision.HIGH
    )
    return panel.reshape(examples, blocks_here * PR * PS).astype(jnp.bfloat16)


def on_device(left_feat, right_feat, embed, conv_w, head, assign, proj_delta, proj_input):
    group = ("zh", "core", "col")
    n_group = lax.axis_size(group)
    n_zh = lax.axis_size("zh")
    n_core = lax.axis_size("core")
    n_col = lax.axis_size("col")
    n_y = lax.axis_size("y")
    n_blk = lax.axis_size("pblk")
    left_each = left_feat.shape[0]
    right_each = right_feat.shape[2]
    right_local = right_feat.reshape(right_each, right_feat.shape[3])
    own_features = jnp.concatenate([left_feat, right_local], 0)
    panel = panels(own_features, embed, conv_w, head, assign, proj_delta, proj_input)
    own = panel.shape[0]
    width = panel.shape[1] // n_group
    sliced = panel.reshape(own, n_group, width)
    spread = lax.all_to_all(sliced, group, split_axis=1, concat_axis=0, tiled=True)
    spread = spread.reshape(n_group, own, width)
    left_part = spread[:, :left_each].reshape(n_group * left_each, width)
    right_part = spread[:, left_each:].reshape(n_group * right_each, width)
    right_tile = lax.all_gather(right_part, "y", axis=0, tiled=True)
    up = [(j, (j + 1) % n_blk) for j in range(n_blk)]
    down = [(j, (j - 1) % n_blk) for j in range(n_blk)]
    from_below = lax.ppermute(left_part, "pblk", up)
    from_above = lax.ppermute(left_part, "pblk", down)
    half = left_part.shape[0] // 2
    far_low = lax.ppermute(from_below[:half], "pblk", up)
    far_high = lax.ppermute(from_above[half:], "pblk", down)
    far = jnp.concatenate([far_low, far_high], 0)
    left_tile = jnp.stack([far, from_below, left_part, from_above])
    left_tile = left_tile.reshape(n_blk, n_zh * n_core, n_col, left_each, width)
    left_tile = jnp.transpose(left_tile, (1, 2, 0, 3, 4)).reshape(-1, width)
    right_tile = right_tile.reshape(n_y, n_zh, n_core, n_col, right_each, width)
    right_tile = jnp.transpose(right_tile, (3, 1, 0, 2, 4, 5)).reshape(-1, width)
    partial_t = jnp.einsum("rk,lk->rl", right_tile, left_tile, preferred_element_type=jnp.float32)
    chunks = partial_t.reshape(n_col, partial_t.shape[0] // n_col, n_zh * n_core, -1)
    chunks = jnp.transpose(chunks, (2, 0, 1, 3)).reshape(n_group, chunks.shape[1], chunks.shape[3])
    received = lax.all_to_all(chunks, group, split_axis=0, concat_axis=0, tiled=True)
    block = jnp.sum(received, axis=0).T
    block = block.reshape(n_col, n_blk, left_each, block.shape[1])
    block = jnp.roll(block, lax.axis_index("pblk") - 2, axis=1)
    return block.reshape(-1, block.shape[3])


def solution(mesh):
    n_row = mesh.shape["row"]
    fine = Mesh(
        mesh.devices.reshape(2, 4, n_row // 8, mesh.shape["col"], mesh.shape["pblk"]),
        ("zh", "y", "core", "col", "pblk"),
    )
    rows = ("zh", "y", "core")
    placed = (
        P((*rows, "col", "pblk"), None),
        P("col", "pblk", rows, None),
        P(),
        P(),
        P(),
        P(),
        P(),
        P(),
    )
    return jax.shard_map(
        on_device, mesh=fine, in_specs=placed, out_specs=P(rows, ("col", "pblk")), check_vma=False
    )
```

```python
import jax
import jax.numpy as jnp
from jax import lax
from jax.sharding import Mesh, PartitionSpec as P

SEQ = 64
NFEAT = 4
VOCAB = 256
LAYERS = 8
PR = 128
PS = 128


def shift_wide(inputs):
    blank = jnp.zeros_like(inputs[:, :1])
    earlier = jnp.concatenate([blank, inputs[:, :-1]], 1)
    later_cells = jnp.concatenate([inputs[:, 1:], blank], 1)
    return jnp.concatenate([earlier, inputs, later_cells], 2)


def panels(features, embed, conv_w, head, assign, proj_delta, proj_input):
    examples = features.shape[0]
    blocks_here = proj_delta.shape[0]
    offsets = jnp.arange(NFEAT, dtype=jnp.int32) * VOCAB
    table_rows = features.reshape(examples, SEQ, NFEAT) + offsets
    table_ids = jnp.arange(NFEAT * VOCAB, dtype=jnp.int32)
    onehot = (table_rows[:, :, 0:1] == table_ids).astype(jnp.bfloat16)
    for field in range(1, NFEAT):
        onehot = onehot + (table_rows[:, :, field : field + 1] == table_ids).astype(jnp.bfloat16)
    hidden = jnp.einsum("esv,vc->esc", onehot, embed, preferred_element_type=jnp.float32)
    wides = []
    pres = []
    for layer in range(LAYERS):
        wide_input = shift_wide(hidden.astype(jnp.bfloat16))
        pre_act = jnp.einsum(
            "esk,kc->esc", wide_input, conv_w[layer], preferred_element_type=jnp.float32
        )
        wides.append(wide_input)
        pres.append(pre_act)
        hidden = hidden + jax.nn.silu(pre_act)
    grad_h = jnp.broadcast_to(head / SEQ, hidden.shape)
    delta_sides = [None] * LAYERS
    input_sides = [None] * LAYERS
    for layer in range(LAYERS - 1, -1, -1):
        pre_act = pres[layer]
        sigmoid_z = jax.nn.sigmoid(pre_act)
        delta_low = (grad_h * sigmoid_z * (1.0 + pre_act * (1.0 - sigmoid_z))).astype(jnp.bfloat16)
        delta_sides[layer] = jnp.einsum(
            "esc,cr->esr", delta_low, proj_delta[assign[layer]], preferred_element_type=jnp.float32
        )
        input_sides[layer] = jnp.einsum(
            "esk,kt->est", wides[layer], proj_input[assign[layer]], preferred_element_type=jnp.float32
        )
        if layer > 0:
            back_wide = jnp.einsum(
                "esc,kc->esk", delta_low, conv_w[layer], preferred_element_type=jnp.float32
            )
            width = grad_h.shape[2]
            first_third = back_wide[:, :, :width]
            last_third = back_wide[:, :, 2 * width :]
            blank = jnp.zeros_like(first_third[:, :1])
            grad_input = back_wide[:, :, width : 2 * width]
            grad_input = grad_input + jnp.concatenate([first_third[:, 1:], blank], 1)
            grad_input = grad_input + jnp.concatenate([blank, last_third[:, :-1]], 1)
            grad_h = grad_h + grad_input
    layer_ids = jnp.arange(LAYERS, dtype=jnp.int32)
    same_before = jnp.sum(
        (assign[None, :] == assign[:, None]) & (layer_ids[None, :] < layer_ids[:, None]), axis=1
    )
    slot = assign * (LAYERS // blocks_here) + same_before
    order = jnp.sum(
        jnp.where(slot[None, :] == layer_ids[:, None], layer_ids[None, :], 0), axis=1
    )
    delta_stack = jnp.stack(delta_sides)[order]
    input_stack = jnp.stack(input_sides)[order]
    per_block = LAYERS // blocks_here
    delta_stack = delta_stack.reshape(blocks_here, per_block, examples, SEQ, PR)
    input_stack = input_stack.reshape(blocks_here, per_block, examples, SEQ, PS)
    panel = jnp.einsum(
        "bjesr,bjest->ebrt", delta_stack, input_stack, precision=lax.Precision.HIGH
    )
    return panel.reshape(examples, blocks_here * PR * PS).astype(jnp.bfloat16)


def on_device(left_feat, right_feat, embed, conv_w, head, assign, proj_delta, proj_input):
    group = ("zh", "core", "col")
    n_group = lax.axis_size(group)
    n_zh = lax.axis_size("zh")
    n_core = lax.axis_size("core")
    n_col = lax.axis_size("col")
    n_y = lax.axis_size("y")
    n_blk = lax.axis_size("pblk")
    left_each = left_feat.shape[0]
    right_each = right_feat.shape[2]
    right_local = right_feat.reshape(right_each, right_feat.shape[3])
    own_features = jnp.concatenate([left_feat, right_local], 0)
    panel = panels(own_features, embed, conv_w, head, assign, proj_delta, proj_input)
    own = panel.shape[0]
    width = panel.shape[1] // n_group
    sliced = panel.reshape(own, n_group, width)
    left_part = lax.all_to_all(sliced[:left_each], group, split_axis=1, concat_axis=0, tiled=True)
    left_part = left_part.reshape(n_group * left_each, width)
    up = [(j, (j + 1) % n_blk) for j in range(n_blk)]
    down = [(j, (j - 1) % n_blk) for j in range(n_blk)]
    from_below = lax.ppermute(left_part, "pblk", up)
    from_above = lax.ppermute(left_part, "pblk", down)
    half = left_part.shape[0] // 2
    far_low = lax.ppermute(from_below[:half], "pblk", up)
    far_high = lax.ppermute(from_above[half:], "pblk", down)
    far = jnp.concatenate([far_low, far_high], 0)
    right_part = lax.all_to_all(sliced[left_each:], group, split_axis=1, concat_axis=0, tiled=True)
    right_part = right_part.reshape(n_group * right_each, width)
    right_tile = lax.all_gather(right_part, "y", axis=0, tiled=True)
    left_tile = jnp.stack([far, from_below, left_part, from_above])
    left_tile = left_tile.reshape(n_blk, n_zh * n_core, n_col, left_each, width)
    left_tile = jnp.transpose(left_tile, (1, 2, 0, 3, 4)).reshape(-1, width)
    right_tile = right_tile.reshape(n_y, n_zh, n_core, n_col, right_each, width)
    right_tile = jnp.transpose(right_tile, (3, 1, 0, 2, 4, 5)).reshape(-1, width)
    partial_t = jnp.einsum("rk,lk->rl", right_tile, left_tile, preferred_element_type=jnp.float32)
    chunks = partial_t.reshape(n_col, partial_t.shape[0] // n_col, n_zh * n_core, -1)
    chunks = jnp.transpose(chunks, (2, 0, 1, 3)).reshape(n_group, chunks.shape[1], chunks.shape[3])
    received = lax.all_to_all(chunks, group, split_axis=0, concat_axis=0, tiled=True)
    block = jnp.sum(received, axis=0).T
    block = block.reshape(n_col, n_blk, left_each, block.shape[1])
    block = jnp.roll(block, lax.axis_index("pblk") - 2, axis=1)
    return block.reshape(-1, block.shape[3])


def solution(mesh):
    n_row = mesh.shape["row"]
    fine = Mesh(
        mesh.devices.reshape(2, 4, n_row // 8, mesh.shape["col"], mesh.shape["pblk"]),
        ("zh", "y", "core", "col", "pblk"),
    )
    rows = ("zh", "y", "core")
    placed = (
        P((*rows, "col", "pblk"), None),
        P("col", "pblk", rows, None),
        P(),
        P(),
        P(),
        P(),
        P(),
        P(),
    )
    return jax.shard_map(
        on_device, mesh=fine, in_specs=placed, out_specs=P(rows, ("col", "pblk")), check_vma=False
    )
```

```python
import jax
import jax.numpy as jnp
from jax import lax
from jax.sharding import Mesh, PartitionSpec as P

SEQ = 64
NFEAT = 4
VOCAB = 256
LAYERS = 8
PR = 128
PS = 128


def shift_wide(inputs):
    blank = jnp.zeros_like(inputs[:, :1])
    earlier = jnp.concatenate([blank, inputs[:, :-1]], 1)
    later_cells = jnp.concatenate([inputs[:, 1:], blank], 1)
    return jnp.concatenate([earlier, inputs, later_cells], 2)


def panels(features, embed, conv_w, head, assign, proj_delta, proj_input):
    examples = features.shape[0]
    blocks_here = proj_delta.shape[0]
    offsets = jnp.arange(NFEAT, dtype=jnp.int32) * VOCAB
    table_rows = features.reshape(examples, SEQ, NFEAT) + offsets
    table_ids = jnp.arange(NFEAT * VOCAB, dtype=jnp.int32)
    onehot = (table_rows[:, :, 0:1] == table_ids).astype(jnp.bfloat16)
    for field in range(1, NFEAT):
        onehot = onehot + (table_rows[:, :, field : field + 1] == table_ids).astype(jnp.bfloat16)
    hidden = jnp.einsum("esv,vc->esc", onehot, embed, preferred_element_type=jnp.float32)
    wides = []
    pres = []
    for layer in range(LAYERS):
        wide_input = shift_wide(hidden.astype(jnp.bfloat16))
        pre_act = jnp.einsum(
            "esk,kc->esc", wide_input, conv_w[layer], preferred_element_type=jnp.float32
        )
        wides.append(wide_input)
        pres.append(pre_act)
        hidden = hidden + jax.nn.silu(pre_act)
    grad_h = jnp.broadcast_to(head / SEQ, hidden.shape)
    delta_sides = [None] * LAYERS
    input_sides = [None] * LAYERS
    for layer in range(LAYERS - 1, -1, -1):
        pre_act = pres[layer]
        sigmoid_z = jax.nn.sigmoid(pre_act)
        delta_low = (grad_h * sigmoid_z * (1.0 + pre_act * (1.0 - sigmoid_z))).astype(jnp.bfloat16)
        delta_sides[layer] = jnp.einsum(
            "esc,cr->esr", delta_low, proj_delta[assign[layer]], preferred_element_type=jnp.float32
        )
        input_sides[layer] = jnp.einsum(
            "esk,kt->est", wides[layer], proj_input[assign[layer]], preferred_element_type=jnp.float32
        )
        if layer > 0:
            back_wide = jnp.einsum(
                "esc,kc->esk", delta_low, conv_w[layer], preferred_element_type=jnp.float32
            )
            width = grad_h.shape[2]
            first_third = back_wide[:, :, :width]
            last_third = back_wide[:, :, 2 * width :]
            blank = jnp.zeros_like(first_third[:, :1])
            grad_input = back_wide[:, :, width : 2 * width]
            grad_input = grad_input + jnp.concatenate([first_third[:, 1:], blank], 1)
            grad_input = grad_input + jnp.concatenate([blank, last_third[:, :-1]], 1)
            grad_h = grad_h + grad_input
    layer_ids = jnp.arange(LAYERS, dtype=jnp.int32)
    same_before = jnp.sum(
        (assign[None, :] == assign[:, None]) & (layer_ids[None, :] < layer_ids[:, None]), axis=1
    )
    slot = assign * (LAYERS // blocks_here) + same_before
    order = jnp.sum(
        jnp.where(slot[None, :] == layer_ids[:, None], layer_ids[None, :], 0), axis=1
    )
    delta_stack = jnp.stack(delta_sides)[order]
    input_stack = jnp.stack(input_sides)[order]
    per_block = LAYERS // blocks_here
    delta_stack = delta_stack.reshape(blocks_here, per_block, examples, SEQ, PR)
    input_stack = input_stack.reshape(blocks_here, per_block, examples, SEQ, PS)
    panel = jnp.einsum(
        "bjesr,bjest->ebrt", delta_stack, input_stack, precision=lax.Precision.HIGH
    )
    return panel.reshape(examples, blocks_here * PR * PS).astype(jnp.bfloat16)


def on_device(left_feat, right_feat, embed, conv_w, head, assign, proj_delta, proj_input):
    group = ("zh", "core", "col")
    n_group = lax.axis_size(group)
    n_zh = lax.axis_size("zh")
    n_core = lax.axis_size("core")
    n_col = lax.axis_size("col")
    n_y = lax.axis_size("y")
    n_blk = lax.axis_size("pblk")
    left_each = left_feat.shape[0]
    right_each = right_feat.shape[2]
    right_local = right_feat.reshape(right_each, right_feat.shape[3])
    own_features = jnp.concatenate([left_feat, right_local], 0)
    panel = panels(own_features, embed, conv_w, head, assign, proj_delta, proj_input)
    own = panel.shape[0]
    width = panel.shape[1] // n_group
    sliced = panel.reshape(own, n_group, width)
    left_part = lax.all_to_all(sliced[:left_each], group, split_axis=1, concat_axis=0, tiled=True)
    left_part = left_part.reshape(n_group * left_each, width)
    left_tile = lax.all_gather(left_part, "pblk", axis=0, tiled=True)
    left_part, right_sliced = lax.optimization_barrier((left_part, sliced[left_each:]))
    right_part = lax.all_to_all(right_sliced, group, split_axis=1, concat_axis=0, tiled=True)
    right_part = right_part.reshape(n_group * right_each, width)
    up = [(j, (j + 1) % n_y) for j in range(n_y)]
    down = [(j, (j - 1) % n_y) for j in range(n_y)]
    from_below = lax.ppermute(right_part, "y", up)
    from_above = lax.ppermute(right_part, "y", down)
    half = right_part.shape[0] // 2
    far_low = lax.ppermute(from_below[:half], "y", up)
    far_high = lax.ppermute(from_above[half:], "y", down)
    far = jnp.concatenate([far_low, far_high], 0)
    right_tile = jnp.stack([far, from_below, right_part, from_above])
    left_tile = left_tile.reshape(n_blk, n_zh * n_core, n_col, left_each, width)
    left_tile = jnp.transpose(left_tile, (1, 2, 0, 3, 4)).reshape(-1, width)
    right_tile = right_tile.reshape(n_y, n_zh, n_core, n_col, right_each, width)
    right_tile = jnp.transpose(right_tile, (3, 1, 0, 2, 4, 5)).reshape(-1, width)
    partial_t = jnp.einsum("rk,lk->rl", right_tile, left_tile, preferred_element_type=jnp.float32)
    chunks = partial_t.reshape(n_col, partial_t.shape[0] // n_col, n_zh * n_core, -1)
    chunks = jnp.transpose(chunks, (2, 0, 1, 3)).reshape(n_group, chunks.shape[1], chunks.shape[3])
    received = lax.all_to_all(chunks, group, split_axis=0, concat_axis=0, tiled=True)
    block = jnp.sum(received, axis=0).T
    block = block.reshape(block.shape[0], n_zh, n_y, n_core * right_each)
    block = jnp.roll(block, lax.axis_index("y") - 2, axis=2)
    return block.reshape(block.shape[0], -1)


def solution(mesh):
    n_row = mesh.shape["row"]
    fine = Mesh(
        mesh.devices.reshape(2, 4, n_row // 8, mesh.shape["col"], mesh.shape["pblk"]),
        ("zh", "y", "core", "col", "pblk"),
    )
    rows = ("zh", "y", "core")
    placed = (
        P((*rows, "col", "pblk"), None),
        P("col", "pblk", rows, None),
        P(),
        P(),
        P(),
        P(),
        P(),
        P(),
    )
    return jax.shard_map(
        on_device, mesh=fine, in_specs=placed, out_specs=P(rows, ("col", "pblk")), check_vma=False
    )
```

```python
import jax
import jax.numpy as jnp
from jax import lax
from jax.sharding import Mesh, PartitionSpec as P

SEQ = 64
NFEAT = 4
VOCAB = 256
LAYERS = 8
PR = 128
PS = 128


def shift_wide(inputs):
    blank = jnp.zeros_like(inputs[:, :1])
    earlier = jnp.concatenate([blank, inputs[:, :-1]], 1)
    later_cells = jnp.concatenate([inputs[:, 1:], blank], 1)
    return jnp.concatenate([earlier, inputs, later_cells], 2)


def panels(features, embed, conv_w, head, assign, proj_delta, proj_input):
    examples = features.shape[0]
    blocks_here = proj_delta.shape[0]
    offsets = jnp.arange(NFEAT, dtype=jnp.int32) * VOCAB
    table_rows = features.reshape(examples, SEQ, NFEAT) + offsets
    table_ids = jnp.arange(NFEAT * VOCAB, dtype=jnp.int32)
    onehot = (table_rows[:, :, 0:1] == table_ids).astype(jnp.bfloat16)
    for field in range(1, NFEAT):
        onehot = onehot + (table_rows[:, :, field : field + 1] == table_ids).astype(jnp.bfloat16)
    hidden = jnp.einsum("esv,vc->esc", onehot, embed, preferred_element_type=jnp.float32)
    wides = []
    pres = []
    for layer in range(LAYERS):
        wide_input = shift_wide(hidden.astype(jnp.bfloat16))
        pre_act = jnp.einsum(
            "esk,kc->esc", wide_input, conv_w[layer], preferred_element_type=jnp.float32
        )
        wides.append(wide_input)
        pres.append(pre_act)
        hidden = hidden + jax.nn.silu(pre_act)
    grad_h = jnp.broadcast_to(head / SEQ, hidden.shape)
    delta_sides = [None] * LAYERS
    input_sides = [None] * LAYERS
    for layer in range(LAYERS - 1, -1, -1):
        pre_act = pres[layer]
        sigmoid_z = jax.nn.sigmoid(pre_act)
        delta_low = (grad_h * sigmoid_z * (1.0 + pre_act * (1.0 - sigmoid_z))).astype(jnp.bfloat16)
        delta_sides[layer] = jnp.einsum(
            "esc,cr->esr", delta_low, proj_delta[assign[layer]], preferred_element_type=jnp.float32
        )
        input_sides[layer] = jnp.einsum(
            "esk,kt->est", wides[layer], proj_input[assign[layer]], preferred_element_type=jnp.float32
        )
        if layer > 0:
            back_wide = jnp.einsum(
                "esc,kc->esk", delta_low, conv_w[layer], preferred_element_type=jnp.float32
            )
            width = grad_h.shape[2]
            first_third = back_wide[:, :, :width]
            last_third = back_wide[:, :, 2 * width :]
            blank = jnp.zeros_like(first_third[:, :1])
            grad_input = back_wide[:, :, width : 2 * width]
            grad_input = grad_input + jnp.concatenate([first_third[:, 1:], blank], 1)
            grad_input = grad_input + jnp.concatenate([blank, last_third[:, :-1]], 1)
            grad_h = grad_h + grad_input
    layer_ids = jnp.arange(LAYERS, dtype=jnp.int32)
    same_before = jnp.sum(
        (assign[None, :] == assign[:, None]) & (layer_ids[None, :] < layer_ids[:, None]), axis=1
    )
    slot = assign * (LAYERS // blocks_here) + same_before
    order = jnp.sum(
        jnp.where(slot[None, :] == layer_ids[:, None], layer_ids[None, :], 0), axis=1
    )
    delta_stack = jnp.stack(delta_sides)[order]
    input_stack = jnp.stack(input_sides)[order]
    per_block = LAYERS // blocks_here
    delta_stack = delta_stack.reshape(blocks_here, per_block, examples, SEQ, PR)
    input_stack = input_stack.reshape(blocks_here, per_block, examples, SEQ, PS)
    panel = jnp.einsum(
        "bjesr,bjest->ebrt", delta_stack, input_stack, precision=lax.Precision.HIGH
    )
    return panel.reshape(examples, blocks_here * PR * PS).astype(jnp.bfloat16)


def spread(sliced):
    rows, _, width = sliced.shape
    n_core = lax.axis_size("core")
    ring = lax.axis_size(("zh", "col"))
    pair = lax.all_to_all(
        sliced.reshape(rows, n_core, ring, width), "core", split_axis=1, concat_axis=0, tiled=True
    )
    pair = pair.reshape(n_core * rows, ring, width)
    out = lax.all_to_all(pair, ("zh", "col"), split_axis=1, concat_axis=0, tiled=True)
    return out.reshape(ring * n_core * rows, width)


def on_device(left_feat, right_feat, embed, conv_w, head, assign, proj_delta, proj_input):
    group = ("zh", "core", "col")
    n_group = lax.axis_size(group)
    n_zh = lax.axis_size("zh")
    n_core = lax.axis_size("core")
    n_col = lax.axis_size("col")
    n_y = lax.axis_size("y")
    n_blk = lax.axis_size("pblk")
    left_each = left_feat.shape[0]
    right_each = right_feat.shape[2]
    right_local = right_feat.reshape(right_each, right_feat.shape[3])
    own_features = jnp.concatenate([left_feat, right_local], 0)
    panel = panels(own_features, embed, conv_w, head, assign, proj_delta, proj_input)
    own = panel.shape[0]
    width = panel.shape[1] // n_group
    sliced = panel.reshape(own, n_group, width)
    left_part = spread(sliced[:left_each])
    left_tile = lax.all_gather(left_part, "pblk", axis=0, tiled=True)
    left_part, right_sliced = lax.optimization_barrier((left_part, sliced[left_each:]))
    right_part = spread(right_sliced)
    up = [(j, (j + 1) % n_y) for j in range(n_y)]
    down = [(j, (j - 1) % n_y) for j in range(n_y)]
    from_below = lax.ppermute(right_part, "y", up)
    from_above = lax.ppermute(right_part, "y", down)
    half = right_part.shape[0] // 2
    far_low = lax.ppermute(from_below[:half], "y", up)
    far_high = lax.ppermute(from_above[half:], "y", down)
    far = jnp.concatenate([far_low, far_high], 0)
    right_tile = jnp.stack([far, from_below, right_part, from_above])
    left_tile = left_tile.reshape(n_blk, n_zh, n_col, n_core, left_each, width)
    left_tile = jnp.transpose(left_tile, (1, 3, 2, 0, 4, 5)).reshape(-1, width)
    right_tile = right_tile.reshape(n_y, n_zh, n_col, n_core, right_each, width)
    right_tile = jnp.transpose(right_tile, (2, 1, 0, 3, 4, 5)).reshape(-1, width)
    partial_t = jnp.einsum("rk,lk->rl", right_tile, left_tile, preferred_element_type=jnp.float32)
    chunks = partial_t.reshape(n_col, partial_t.shape[0] // n_col, n_zh * n_core, -1)
    chunks = jnp.transpose(chunks, (2, 0, 1, 3)).reshape(n_group, chunks.shape[1], chunks.shape[3])
    received = lax.all_to_all(chunks, group, split_axis=0, concat_axis=0, tiled=True)
    block = jnp.sum(received, axis=0).T
    block = block.reshape(block.shape[0], n_zh, n_y, n_core * right_each)
    block = jnp.roll(block, lax.axis_index("y") - 2, axis=2)
    return block.reshape(block.shape[0], -1)


def solution(mesh):
    n_row = mesh.shape["row"]
    fine = Mesh(
        mesh.devices.reshape(2, 4, n_row // 8, mesh.shape["col"], mesh.shape["pblk"]),
        ("zh", "y", "core", "col", "pblk"),
    )
    rows = ("zh", "y", "core")
    placed = (
        P((*rows, "col", "pblk"), None),
        P("col", "pblk", rows, None),
        P(),
        P(),
        P(),
        P(),
        P(),
        P(),
    )
    return jax.shard_map(
        on_device, mesh=fine, in_specs=placed, out_specs=P(rows, ("col", "pblk")), check_vma=False
    )
```

```python
import jax
import jax.numpy as jnp
from jax import lax
from jax.sharding import Mesh, PartitionSpec as P

SEQ = 64
NFEAT = 4
VOCAB = 256
LAYERS = 8
PR = 128
PS = 128


def shift_wide(inputs):
    blank = jnp.zeros_like(inputs[:, :1])
    earlier = jnp.concatenate([blank, inputs[:, :-1]], 1)
    later_cells = jnp.concatenate([inputs[:, 1:], blank], 1)
    return jnp.concatenate([earlier, inputs, later_cells], 2)


def panels(features, embed, conv_w, head, assign, proj_delta, proj_input):
    examples = features.shape[0]
    blocks_here = proj_delta.shape[0]
    offsets = jnp.arange(NFEAT, dtype=jnp.int32) * VOCAB
    table_rows = features.reshape(examples, SEQ, NFEAT) + offsets
    table_ids = jnp.arange(NFEAT * VOCAB, dtype=jnp.int32)
    onehot = (table_rows[:, :, 0:1] == table_ids).astype(jnp.bfloat16)
    for field in range(1, NFEAT):
        onehot = onehot + (table_rows[:, :, field : field + 1] == table_ids).astype(jnp.bfloat16)
    hidden = jnp.einsum("esv,vc->esc", onehot, embed, preferred_element_type=jnp.float32)
    wides = []
    pres = []
    for layer in range(LAYERS):
        wide_input = shift_wide(hidden.astype(jnp.bfloat16))
        pre_act = jnp.einsum(
            "esk,kc->esc", wide_input, conv_w[layer], preferred_element_type=jnp.float32
        )
        wides.append(wide_input)
        pres.append(pre_act)
        hidden = hidden + jax.nn.silu(pre_act)
    grad_h = jnp.broadcast_to(head / SEQ, hidden.shape)
    delta_sides = [None] * LAYERS
    input_sides = [None] * LAYERS
    for layer in range(LAYERS - 1, -1, -1):
        pre_act = pres[layer]
        sigmoid_z = jax.nn.sigmoid(pre_act)
        delta_low = (grad_h * sigmoid_z * (1.0 + pre_act * (1.0 - sigmoid_z))).astype(jnp.bfloat16)
        delta_sides[layer] = jnp.einsum(
            "esc,cr->esr", delta_low, proj_delta[assign[layer]], preferred_element_type=jnp.float32
        )
        input_sides[layer] = jnp.einsum(
            "esk,kt->est", wides[layer], proj_input[assign[layer]], preferred_element_type=jnp.float32
        )
        if layer > 0:
            back_wide = jnp.einsum(
                "esc,kc->esk", delta_low, conv_w[layer], preferred_element_type=jnp.float32
            )
            width = grad_h.shape[2]
            first_third = back_wide[:, :, :width]
            last_third = back_wide[:, :, 2 * width :]
            blank = jnp.zeros_like(first_third[:, :1])
            grad_input = back_wide[:, :, width : 2 * width]
            grad_input = grad_input + jnp.concatenate([first_third[:, 1:], blank], 1)
            grad_input = grad_input + jnp.concatenate([blank, last_third[:, :-1]], 1)
            grad_h = grad_h + grad_input
    layer_ids = jnp.arange(LAYERS, dtype=jnp.int32)
    same_before = jnp.sum(
        (assign[None, :] == assign[:, None]) & (layer_ids[None, :] < layer_ids[:, None]), axis=1
    )
    slot = assign * (LAYERS // blocks_here) + same_before
    order = jnp.sum(
        jnp.where(slot[None, :] == layer_ids[:, None], layer_ids[None, :], 0), axis=1
    )
    pick = (order[:, None] == layer_ids[None, :]).astype(jnp.float32)
    delta_stack = jnp.einsum(
        "jl,lesr->jesr", pick, jnp.stack(delta_sides), precision=lax.Precision.HIGHEST
    )
    input_stack = jnp.einsum(
        "jl,lest->jest", pick, jnp.stack(input_sides), precision=lax.Precision.HIGHEST
    )
    per_block = LAYERS // blocks_here
    delta_stack = delta_stack.reshape(blocks_here, per_block, examples, SEQ, PR)
    input_stack = input_stack.reshape(blocks_here, per_block, examples, SEQ, PS)
    panel = jnp.einsum(
        "bjesr,bjest->ebrt", delta_stack, input_stack, precision=lax.Precision.HIGH
    )
    return panel.reshape(examples, blocks_here * PR * PS).astype(jnp.bfloat16)


def on_device(left_feat, right_feat, embed, conv_w, head, assign, proj_delta, proj_input):
    group = ("zh", "core", "col")
    n_group = lax.axis_size(group)
    n_zh = lax.axis_size("zh")
    n_core = lax.axis_size("core")
    n_col = lax.axis_size("col")
    n_y = lax.axis_size("y")
    n_blk = lax.axis_size("pblk")
    left_each = left_feat.shape[0]
    right_each = right_feat.shape[2]
    right_local = right_feat.reshape(right_each, right_feat.shape[3])
    own_features = jnp.concatenate([left_feat, right_local], 0)
    panel = panels(own_features, embed, conv_w, head, assign, proj_delta, proj_input)
    own = panel.shape[0]
    width = panel.shape[1] // n_group
    sliced = panel.reshape(own, n_group, width)
    left_part = lax.all_to_all(sliced[:left_each], group, split_axis=1, concat_axis=0, tiled=True)
    left_part = left_part.reshape(n_group * left_each, width)
    left_tile = lax.all_gather(left_part, "pblk", axis=0, tiled=True)
    left_part, right_sliced = lax.optimization_barrier((left_part, sliced[left_each:]))
    right_part = lax.all_to_all(right_sliced, group, split_axis=1, concat_axis=0, tiled=True)
    right_part = right_part.reshape(n_group * right_each, width)
    up = [(j, (j + 1) % n_y) for j in range(n_y)]
    down = [(j, (j - 1) % n_y) for j in range(n_y)]
    from_below = lax.ppermute(right_part, "y", up)
    from_above = lax.ppermute(right_part, "y", down)
    half = right_part.shape[0] // 2
    far_low = lax.ppermute(from_below[:half], "y", up)
    far_high = lax.ppermute(from_above[half:], "y", down)
    far = jnp.concatenate([far_low, far_high], 0)
    right_tile = jnp.stack([far, from_below, right_part, from_above])
    left_tile = left_tile.reshape(n_blk, n_zh * n_core, n_col, left_each, width)
    left_tile = jnp.transpose(left_tile, (1, 2, 0, 3, 4)).reshape(-1, width)
    right_tile = right_tile.reshape(n_y, n_zh, n_core, n_col, right_each, width)
    right_tile = jnp.transpose(right_tile, (3, 1, 0, 2, 4, 5)).reshape(-1, width)
    partial_t = jnp.einsum("rk,lk->rl", right_tile, left_tile, preferred_element_type=jnp.float32)
    chunks = partial_t.reshape(n_col, partial_t.shape[0] // n_col, n_zh * n_core, -1)
    chunks = jnp.transpose(chunks, (2, 0, 1, 3)).reshape(n_group, chunks.shape[1], chunks.shape[3])
    received = lax.all_to_all(chunks, group, split_axis=0, concat_axis=0, tiled=True)
    block = jnp.sum(received, axis=0).T
    block = block.reshape(block.shape[0], n_zh, n_y, n_core * right_each)
    block = jnp.roll(block, lax.axis_index("y") - 2, axis=2)
    return block.reshape(block.shape[0], -1)


def solution(mesh):
    n_row = mesh.shape["row"]
    fine = Mesh(
        mesh.devices.reshape(2, 4, n_row // 8, mesh.shape["col"], mesh.shape["pblk"]),
        ("zh", "y", "core", "col", "pblk"),
    )
    rows = ("zh", "y", "core")
    placed = (
        P((*rows, "col", "pblk"), None),
        P("col", "pblk", rows, None),
        P(),
        P(),
        P(),
        P(),
        P(),
        P(),
    )
    return jax.shard_map(
        on_device, mesh=fine, in_specs=placed, out_specs=P(rows, ("col", "pblk")), check_vma=False
    )
```

```python
import jax
import jax.numpy as jnp
from jax import lax
from jax.sharding import Mesh, PartitionSpec as P

SEQ = 64
NFEAT = 4
VOCAB = 256
LAYERS = 8
PR = 128
PS = 128


def shift_wide(inputs):
    blank = jnp.zeros_like(inputs[:, :1])
    earlier = jnp.concatenate([blank, inputs[:, :-1]], 1)
    later_cells = jnp.concatenate([inputs[:, 1:], blank], 1)
    return jnp.concatenate([earlier, inputs, later_cells], 2)


def panels(features, embed, conv_w, head, assign, proj_delta, proj_input):
    examples = features.shape[0]
    blocks_here = proj_delta.shape[0]
    offsets = jnp.arange(NFEAT, dtype=jnp.int32) * VOCAB
    table_rows = features.reshape(examples, SEQ, NFEAT) + offsets
    hidden = jnp.sum(jnp.take(embed, table_rows, axis=0).astype(jnp.float32), axis=2)
    wides = []
    pres = []
    for layer in range(LAYERS):
        wide_input = shift_wide(hidden.astype(jnp.bfloat16))
        pre_act = jnp.einsum(
            "esk,kc->esc", wide_input, conv_w[layer], preferred_element_type=jnp.float32
        )
        wides.append(wide_input)
        pres.append(pre_act)
        hidden = hidden + jax.nn.silu(pre_act)
    grad_h = jnp.broadcast_to(head / SEQ, hidden.shape)
    delta_sides = [None] * LAYERS
    input_sides = [None] * LAYERS
    for layer in range(LAYERS - 1, -1, -1):
        pre_act = pres[layer]
        sigmoid_z = jax.nn.sigmoid(pre_act)
        delta_low = (grad_h * sigmoid_z * (1.0 + pre_act * (1.0 - sigmoid_z))).astype(jnp.bfloat16)
        delta_sides[layer] = jnp.einsum(
            "esc,cr->esr", delta_low, proj_delta[assign[layer]], preferred_element_type=jnp.float32
        )
        input_sides[layer] = jnp.einsum(
            "esk,kt->est", wides[layer], proj_input[assign[layer]], preferred_element_type=jnp.float32
        )
        if layer > 0:
            back_wide = jnp.einsum(
                "esc,kc->esk", delta_low, conv_w[layer], preferred_element_type=jnp.float32
            )
            width = grad_h.shape[2]
            first_third = back_wide[:, :, :width]
            last_third = back_wide[:, :, 2 * width :]
            blank = jnp.zeros_like(first_third[:, :1])
            grad_input = back_wide[:, :, width : 2 * width]
            grad_input = grad_input + jnp.concatenate([first_third[:, 1:], blank], 1)
            grad_input = grad_input + jnp.concatenate([blank, last_third[:, :-1]], 1)
            grad_h = grad_h + grad_input
    layer_ids = jnp.arange(LAYERS, dtype=jnp.int32)
    same_before = jnp.sum(
        (assign[None, :] == assign[:, None]) & (layer_ids[None, :] < layer_ids[:, None]), axis=1
    )
    slot = assign * (LAYERS // blocks_here) + same_before
    order = jnp.sum(
        jnp.where(slot[None, :] == layer_ids[:, None], layer_ids[None, :], 0), axis=1
    )
    delta_stack = jnp.stack(delta_sides)[order]
    input_stack = jnp.stack(input_sides)[order]
    per_block = LAYERS // blocks_here
    delta_stack = delta_stack.reshape(blocks_here, per_block, examples, SEQ, PR)
    input_stack = input_stack.reshape(blocks_here, per_block, examples, SEQ, PS)
    panel = jnp.einsum(
        "bjesr,bjest->ebrt", delta_stack, input_stack, precision=lax.Precision.HIGH
    )
    return panel.reshape(examples, blocks_here * PR * PS).astype(jnp.bfloat16)


def on_device(left_feat, right_feat, embed, conv_w, head, assign, proj_delta, proj_input):
    group = ("zh", "core", "col")
    n_group = lax.axis_size(group)
    n_zh = lax.axis_size("zh")
    n_core = lax.axis_size("core")
    n_col = lax.axis_size("col")
    n_y = lax.axis_size("y")
    n_blk = lax.axis_size("pblk")
    left_each = left_feat.shape[0]
    right_each = right_feat.shape[2]
    right_local = right_feat.reshape(right_each, right_feat.shape[3])
    own_features = jnp.concatenate([left_feat, right_local], 0)
    panel = panels(own_features, embed, conv_w, head, assign, proj_delta, proj_input)
    own = panel.shape[0]
    width = panel.shape[1] // n_group
    sliced = panel.reshape(own, n_group, width)
    left_part = lax.all_to_all(sliced[:left_each], group, split_axis=1, concat_axis=0, tiled=True)
    left_part = left_part.reshape(n_group * left_each, width)
    left_tile = lax.all_gather(left_part, "pblk", axis=0, tiled=True)
    left_part, right_sliced = lax.optimization_barrier((left_part, sliced[left_each:]))
    right_part = lax.all_to_all(right_sliced, group, split_axis=1, concat_axis=0, tiled=True)
    right_part = right_part.reshape(n_group * right_each, width)
    up = [(j, (j + 1) % n_y) for j in range(n_y)]
    down = [(j, (j - 1) % n_y) for j in range(n_y)]
    from_below = lax.ppermute(right_part, "y", up)
    from_above = lax.ppermute(right_part, "y", down)
    half = right_part.shape[0] // 2
    far_low = lax.ppermute(from_below[:half], "y", up)
    far_high = lax.ppermute(from_above[half:], "y", down)
    far = jnp.concatenate([far_low, far_high], 0)
    right_tile = jnp.stack([far, from_below, right_part, from_above])
    left_tile = left_tile.reshape(n_blk, n_zh * n_core, n_col, left_each, width)
    left_tile = jnp.transpose(left_tile, (1, 2, 0, 3, 4)).reshape(-1, width)
    right_tile = right_tile.reshape(n_y, n_zh, n_core, n_col, right_each, width)
    right_tile = jnp.transpose(right_tile, (3, 1, 0, 2, 4, 5)).reshape(-1, width)
    partial_t = jnp.einsum("rk,lk->rl", right_tile, left_tile, preferred_element_type=jnp.float32)
    chunks = partial_t.reshape(n_col, partial_t.shape[0] // n_col, n_zh * n_core, -1)
    chunks = jnp.transpose(chunks, (2, 0, 1, 3)).reshape(n_group, chunks.shape[1], chunks.shape[3])
    received = lax.all_to_all(chunks, group, split_axis=0, concat_axis=0, tiled=True)
    block = jnp.sum(received, axis=0).T
    block = block.reshape(block.shape[0], n_zh, n_y, n_core * right_each)
    block = jnp.roll(block, lax.axis_index("y") - 2, axis=2)
    return block.reshape(block.shape[0], -1)


def solution(mesh):
    n_row = mesh.shape["row"]
    fine = Mesh(
        mesh.devices.reshape(2, 4, n_row // 8, mesh.shape["col"], mesh.shape["pblk"]),
        ("zh", "y", "core", "col", "pblk"),
    )
    rows = ("zh", "y", "core")
    placed = (
        P((*rows, "col", "pblk"), None),
        P("col", "pblk", rows, None),
        P(),
        P(),
        P(),
        P(),
        P(),
        P(),
    )
    return jax.shard_map(
        on_device, mesh=fine, in_specs=placed, out_specs=P(rows, ("col", "pblk")), check_vma=False
    )
```

```python
import jax
import jax.numpy as jnp
from jax import lax
from jax.sharding import Mesh, PartitionSpec as P

SEQ = 64
NFEAT = 4
VOCAB = 256
LAYERS = 8
PR = 128
PS = 128


def shift_wide(inputs):
    blank = jnp.zeros_like(inputs[:, :1])
    earlier = jnp.concatenate([blank, inputs[:, :-1]], 1)
    later_cells = jnp.concatenate([inputs[:, 1:], blank], 1)
    return jnp.concatenate([earlier, inputs, later_cells], 2)


def panels(features, embed, conv_w, head, assign, proj_delta, proj_input):
    examples = features.shape[0]
    blocks_here = proj_delta.shape[0]
    offsets = jnp.arange(NFEAT, dtype=jnp.int32) * VOCAB
    table_rows = features.reshape(examples, SEQ, NFEAT) + offsets
    table_ids = jnp.arange(NFEAT * VOCAB, dtype=jnp.int32)
    onehot = (table_rows[:, :, 0:1] == table_ids).astype(jnp.bfloat16)
    for field in range(1, NFEAT):
        onehot = onehot + (table_rows[:, :, field : field + 1] == table_ids).astype(jnp.bfloat16)
    hidden = jnp.einsum("esv,vc->esc", onehot, embed, preferred_element_type=jnp.float32)
    wides = []
    pres = []
    for layer in range(LAYERS):
        wide_input = shift_wide(hidden.astype(jnp.bfloat16))
        pre_act = jnp.einsum(
            "esk,kc->esc", wide_input, conv_w[layer], preferred_element_type=jnp.float32
        )
        wides.append(wide_input)
        pres.append(pre_act)
        hidden = hidden + jax.nn.silu(pre_act)
    grad_h = jnp.broadcast_to(head / SEQ, hidden.shape)
    delta_sides = [None] * LAYERS
    input_sides = [None] * LAYERS
    for layer in range(LAYERS - 1, -1, -1):
        pre_act = pres[layer]
        sigmoid_z = jax.nn.sigmoid(pre_act)
        delta_low = (grad_h * sigmoid_z * (1.0 + pre_act * (1.0 - sigmoid_z))).astype(jnp.bfloat16)
        delta_sides[layer] = jnp.einsum(
            "esc,cr->esr", delta_low, proj_delta[assign[layer]], preferred_element_type=jnp.float32
        )
        input_sides[layer] = jnp.einsum(
            "esk,kt->est", wides[layer], proj_input[assign[layer]], preferred_element_type=jnp.float32
        )
        if layer > 0:
            back_wide = jnp.einsum(
                "esc,kc->esk", delta_low, conv_w[layer], preferred_element_type=jnp.float32
            )
            width = grad_h.shape[2]
            first_third = back_wide[:, :, :width]
            last_third = back_wide[:, :, 2 * width :]
            blank = jnp.zeros_like(first_third[:, :1])
            grad_input = back_wide[:, :, width : 2 * width]
            grad_input = grad_input + jnp.concatenate([first_third[:, 1:], blank], 1)
            grad_input = grad_input + jnp.concatenate([blank, last_third[:, :-1]], 1)
            grad_h = grad_h + grad_input
    layer_ids = jnp.arange(LAYERS, dtype=jnp.int32)
    same_before = jnp.sum(
        (assign[None, :] == assign[:, None]) & (layer_ids[None, :] < layer_ids[:, None]), axis=1
    )
    slot = assign * (LAYERS // blocks_here) + same_before
    order = jnp.sum(
        jnp.where(slot[None, :] == layer_ids[:, None], layer_ids[None, :], 0), axis=1
    )
    delta_stack = jnp.stack(delta_sides)[order]
    input_stack = jnp.stack(input_sides)[order]
    per_block = LAYERS // blocks_here
    delta_stack = delta_stack.reshape(blocks_here, per_block, examples, SEQ, PR)
    input_stack = input_stack.reshape(blocks_here, per_block, examples, SEQ, PS)
    panel = jnp.einsum(
        "bjesr,bjest->ebrt", delta_stack, input_stack, precision=lax.Precision.HIGH
    )
    return panel.reshape(examples, blocks_here * PR * PS).astype(jnp.bfloat16)


def on_device(left_feat, right_feat, embed, conv_w, head, assign, proj_delta, proj_input):
    group = ("zh", "core", "col")
    n_group = lax.axis_size(group)
    n_zh = lax.axis_size("zh")
    n_core = lax.axis_size("core")
    n_col = lax.axis_size("col")
    n_y = lax.axis_size("y")
    n_blk = lax.axis_size("pblk")
    left_each = left_feat.shape[0]
    right_each = right_feat.shape[2]
    right_local = right_feat.reshape(right_each, right_feat.shape[3])
    own_features = jnp.concatenate([left_feat, right_local], 0)
    panel = panels(own_features, embed, conv_w, head, assign, proj_delta, proj_input)
    own = panel.shape[0]
    width = panel.shape[1] // n_group
    sliced = panel.reshape(own, n_group, width)
    left_part = lax.all_to_all(sliced[:left_each], group, split_axis=1, concat_axis=0, tiled=True)
    left_part = left_part.reshape(n_group * left_each, width)
    left_tile = lax.all_gather(left_part, "pblk", axis=0, tiled=True)
    left_part, right_sliced = lax.optimization_barrier((left_part, sliced[left_each:]))
    right_part = lax.all_to_all(right_sliced, group, split_axis=1, concat_axis=0, tiled=True)
    right_part = right_part.reshape(n_group * right_each, width)
    up = [(j, (j + 1) % n_y) for j in range(n_y)]
    down = [(j, (j - 1) % n_y) for j in range(n_y)]
    from_below = lax.ppermute(right_part, "y", up)
    from_above = lax.ppermute(right_part, "y", down)
    half = right_part.shape[0] // 2
    far_low = lax.ppermute(from_below[:half], "y", up)
    far_high = lax.ppermute(from_above[half:], "y", down)
    far = jnp.concatenate([far_low, far_high], 0)
    right_tile = jnp.stack([far, from_below, right_part, from_above])
    left_tile = left_tile.reshape(n_blk, n_zh * n_core, n_col, left_each, width)
    left_tile = jnp.transpose(left_tile, (1, 2, 0, 3, 4)).reshape(-1, width)
    right_tile = right_tile.reshape(n_y, n_zh, n_core, n_col, right_each, width)
    right_tile = jnp.transpose(right_tile, (3, 1, 0, 2, 4, 5)).reshape(-1, width)
    partial_t = jnp.einsum("rk,lk->rl", right_tile, left_tile, preferred_element_type=jnp.float32)
    chunks = partial_t.reshape(n_col, partial_t.shape[0] // n_col, n_zh * n_core, -1)
    chunks = jnp.transpose(chunks, (2, 0, 1, 3)).reshape(n_group, chunks.shape[1], chunks.shape[3])
    chunks = chunks.reshape(n_zh, n_core, n_col, chunks.shape[1], chunks.shape[2])
    mine = lax.axis_index("core")
    swap = [(j, (j + 1) % n_core) for j in range(n_core)]
    for_partner = lax.dynamic_index_in_dim(chunks, 1 - mine, axis=1, keepdims=False)
    kept = lax.dynamic_index_in_dim(chunks, mine, axis=1, keepdims=False)
    paired = kept + lax.ppermute(for_partner, "core", swap)
    paired = paired.reshape(n_zh * n_col, paired.shape[2], paired.shape[3])
    received = lax.all_to_all(paired, ("zh", "col"), split_axis=0, concat_axis=0, tiled=True)
    block = jnp.sum(received, axis=0).T
    block = block.reshape(block.shape[0], n_zh, n_y, n_core * right_each)
    block = jnp.roll(block, lax.axis_index("y") - 2, axis=2)
    return block.reshape(block.shape[0], -1)


def solution(mesh):
    n_row = mesh.shape["row"]
    fine = Mesh(
        mesh.devices.reshape(2, 4, n_row // 8, mesh.shape["col"], mesh.shape["pblk"]),
        ("zh", "y", "core", "col", "pblk"),
    )
    rows = ("zh", "y", "core")
    placed = (
        P((*rows, "col", "pblk"), None),
        P("col", "pblk", rows, None),
        P(),
        P(),
        P(),
        P(),
        P(),
        P(),
    )
    return jax.shard_map(
        on_device, mesh=fine, in_specs=placed, out_specs=P(rows, ("col", "pblk")), check_vma=False
    )
```

```python
import jax
import jax.numpy as jnp
from jax import lax
from jax.sharding import Mesh, PartitionSpec as P

SEQ = 64
NFEAT = 4
VOCAB = 256
LAYERS = 8
PR = 128
PS = 128


def shift_wide(inputs):
    blank = jnp.zeros_like(inputs[:, :1])
    earlier = jnp.concatenate([blank, inputs[:, :-1]], 1)
    later_cells = jnp.concatenate([inputs[:, 1:], blank], 1)
    return jnp.concatenate([earlier, inputs, later_cells], 2)


def panels(features, embed, conv_w, head, assign, proj_delta, proj_input):
    examples = features.shape[0]
    blocks_here = proj_delta.shape[0]
    offsets = jnp.arange(NFEAT, dtype=jnp.int32) * VOCAB
    table_rows = features.reshape(examples, SEQ, NFEAT) + offsets
    table_ids = jnp.arange(NFEAT * VOCAB, dtype=jnp.int32)
    onehot = (table_rows[:, :, 0:1] == table_ids).astype(jnp.bfloat16)
    for field in range(1, NFEAT):
        onehot = onehot + (table_rows[:, :, field : field + 1] == table_ids).astype(jnp.bfloat16)
    hidden = jnp.einsum("esv,vc->esc", onehot, embed, preferred_element_type=jnp.float32)
    wides = []
    pres = []
    for layer in range(LAYERS):
        wide_input = shift_wide(hidden.astype(jnp.bfloat16))
        pre_act = jnp.einsum(
            "esk,kc->esc", wide_input, conv_w[layer], preferred_element_type=jnp.float32
        )
        wides.append(wide_input)
        pres.append(pre_act)
        hidden = hidden + jax.nn.silu(pre_act)
    grad_h = jnp.broadcast_to(head / SEQ, hidden.shape)
    delta_sides = [None] * LAYERS
    input_sides = [None] * LAYERS
    for layer in range(LAYERS - 1, -1, -1):
        pre_act = pres[layer]
        sigmoid_z = jax.nn.sigmoid(pre_act)
        delta_low = (grad_h * sigmoid_z * (1.0 + pre_act * (1.0 - sigmoid_z))).astype(jnp.bfloat16)
        delta_sides[layer] = jnp.einsum(
            "esc,cr->esr", delta_low, proj_delta[assign[layer]], preferred_element_type=jnp.float32
        )
        input_sides[layer] = jnp.einsum(
            "esk,kt->est", wides[layer], proj_input[assign[layer]], preferred_element_type=jnp.float32
        )
        if layer > 0:
            back_wide = jnp.einsum(
                "esc,kc->esk", delta_low, conv_w[layer], preferred_element_type=jnp.float32
            )
            width = grad_h.shape[2]
            first_third = back_wide[:, :, :width]
            last_third = back_wide[:, :, 2 * width :]
            blank = jnp.zeros_like(first_third[:, :1])
            grad_input = back_wide[:, :, width : 2 * width]
            grad_input = grad_input + jnp.concatenate([first_third[:, 1:], blank], 1)
            grad_input = grad_input + jnp.concatenate([blank, last_third[:, :-1]], 1)
            grad_h = grad_h + grad_input
    layer_ids = jnp.arange(LAYERS, dtype=jnp.int32)
    same_before = jnp.sum(
        (assign[None, :] == assign[:, None]) & (layer_ids[None, :] < layer_ids[:, None]), axis=1
    )
    slot = assign * (LAYERS // blocks_here) + same_before
    order = jnp.sum(
        jnp.where(slot[None, :] == layer_ids[:, None], layer_ids[None, :], 0), axis=1
    )
    delta_stack = jnp.stack(delta_sides)[order]
    input_stack = jnp.stack(input_sides)[order]
    per_block = LAYERS // blocks_here
    delta_stack = delta_stack.reshape(blocks_here, per_block, examples, SEQ, PR)
    input_stack = input_stack.reshape(blocks_here, per_block, examples, SEQ, PS)
    panel = jnp.einsum(
        "bjesr,bjest->ebrt", delta_stack, input_stack, precision=lax.Precision.HIGH
    )
    return panel.reshape(examples, blocks_here * PR * PS).astype(jnp.bfloat16)


def on_device(left_feat, right_feat, embed, conv_w, head, assign, proj_delta, proj_input):
    group = ("zh", "core", "col")
    n_group = lax.axis_size(group)
    n_zh = lax.axis_size("zh")
    n_core = lax.axis_size("core")
    n_col = lax.axis_size("col")
    n_y = lax.axis_size("y")
    n_blk = lax.axis_size("pblk")
    left_each = left_feat.shape[0]
    right_each = right_feat.shape[2]
    right_local = right_feat.reshape(right_each, right_feat.shape[3])
    own_features = jnp.concatenate([left_feat, right_local], 0)
    panel = panels(own_features, embed, conv_w, head, assign, proj_delta, proj_input)
    own = panel.shape[0]
    width = panel.shape[1] // n_group
    sliced = panel.reshape(own, n_group, width)
    left_part = lax.all_to_all(sliced[:left_each], group, split_axis=1, concat_axis=0, tiled=True)
    left_part = left_part.reshape(n_group * left_each, width)
    left_tile = lax.all_gather(left_part, "pblk", axis=0, tiled=True)
    left_part, right_sliced = lax.optimization_barrier((left_part, sliced[left_each:]))
    right_part = lax.all_to_all(right_sliced, group, split_axis=1, concat_axis=0, tiled=True)
    right_part = right_part.reshape(n_group * right_each, width)
    up = [(j, (j + 1) % n_y) for j in range(n_y)]
    down = [(j, (j - 1) % n_y) for j in range(n_y)]
    from_below = lax.ppermute(right_part, "y", up)
    from_above = lax.ppermute(right_part, "y", down)
    half = right_part.shape[0] // 2
    far_low = lax.ppermute(from_below[:half], "y", up)
    far_high = lax.ppermute(from_above[half:], "y", down)
    far = jnp.concatenate([far_low, far_high], 0)
    right_tile = jnp.stack([far, from_below, right_part, from_above])
    left_tile = left_tile.reshape(n_blk, n_zh * n_core, n_col, left_each, width)
    left_tile = jnp.transpose(left_tile, (1, 2, 0, 3, 4)).reshape(-1, width)
    right_tile = right_tile.reshape(n_y, n_zh, n_core, n_col, right_each, width)
    right_tile = jnp.transpose(right_tile, (3, 1, 0, 2, 4, 5)).reshape(-1, width)
    partial_t = jnp.einsum("rk,lk->rl", right_tile, left_tile, preferred_element_type=jnp.float32)
    chunks = partial_t.reshape(n_col, partial_t.shape[0] // n_col, n_zh * n_core, -1)
    chunks = jnp.transpose(chunks, (2, 0, 1, 3)).reshape(n_group, chunks.shape[1], chunks.shape[3])
    chunks = chunks.reshape(n_zh, n_core, n_col, chunks.shape[1], chunks.shape[2])
    mine = lax.axis_index("core")
    swap = [(j, (j + 1) % n_core) for j in range(n_core)]
    for_partner = lax.dynamic_index_in_dim(chunks, 1 - mine, axis=1, keepdims=False)
    kept = lax.dynamic_index_in_dim(chunks, mine, axis=1, keepdims=False)
    paired = kept + lax.ppermute(for_partner, "core", swap)
    high = lax.axis_index("zh")
    halves = [(j, (j + 1) % n_zh) for j in range(n_zh)]
    for_far = lax.dynamic_index_in_dim(paired, 1 - high, axis=0, keepdims=False)
    near = lax.dynamic_index_in_dim(paired, high, axis=0, keepdims=False)
    quads = near + lax.ppermute(for_far, "zh", halves)
    received = lax.all_to_all(quads, "col", split_axis=0, concat_axis=0, tiled=True)
    block = jnp.sum(received, axis=0).T
    block = block.reshape(block.shape[0], n_zh, n_y, n_core * right_each)
    block = jnp.roll(block, lax.axis_index("y") - 2, axis=2)
    return block.reshape(block.shape[0], -1)


def solution(mesh):
    n_row = mesh.shape["row"]
    fine = Mesh(
        mesh.devices.reshape(2, 4, n_row // 8, mesh.shape["col"], mesh.shape["pblk"]),
        ("zh", "y", "core", "col", "pblk"),
    )
    rows = ("zh", "y", "core")
    placed = (
        P((*rows, "col", "pblk"), None),
        P("col", "pblk", rows, None),
        P(),
        P(),
        P(),
        P(),
        P(),
        P(),
    )
    return jax.shard_map(
        on_device, mesh=fine, in_specs=placed, out_specs=P(rows, ("col", "pblk")), check_vma=False
    )
```

```python
import jax
import jax.numpy as jnp
from jax import lax
from jax.sharding import Mesh, PartitionSpec as P

SEQ = 64
NFEAT = 4
VOCAB = 256
LAYERS = 8
PR = 128
PS = 128


def shift_wide(inputs):
    blank = jnp.zeros_like(inputs[:, :1])
    earlier = jnp.concatenate([blank, inputs[:, :-1]], 1)
    later_cells = jnp.concatenate([inputs[:, 1:], blank], 1)
    return jnp.concatenate([earlier, inputs, later_cells], 2)


def panels(features, embed, conv_w, head, assign, proj_delta, proj_input):
    examples = features.shape[0]
    blocks_here = proj_delta.shape[0]
    offsets = jnp.arange(NFEAT, dtype=jnp.int32) * VOCAB
    table_rows = features.reshape(examples, SEQ, NFEAT) + offsets
    table_ids = jnp.arange(NFEAT * VOCAB, dtype=jnp.int32)
    onehot = (table_rows[:, :, 0:1] == table_ids).astype(jnp.bfloat16)
    for field in range(1, NFEAT):
        onehot = onehot + (table_rows[:, :, field : field + 1] == table_ids).astype(jnp.bfloat16)
    hidden = jnp.einsum("esv,vc->esc", onehot, embed, preferred_element_type=jnp.float32)
    def forward_layer(hidden, weight):
        wide_input = shift_wide(hidden.astype(jnp.bfloat16))
        pre_act = jnp.einsum("esk,kc->esc", wide_input, weight, preferred_element_type=jnp.float32)
        return hidden + jax.nn.silu(pre_act), (wide_input, pre_act)

    hidden, (wide_stack, pre_stack) = lax.scan(forward_layer, hidden, conv_w)
    wides = [wide_stack[layer] for layer in range(LAYERS)]
    pres = [pre_stack[layer] for layer in range(LAYERS)]
    grad_h = jnp.broadcast_to(head / SEQ, hidden.shape)
    delta_sides = [None] * LAYERS
    input_sides = [None] * LAYERS
    for layer in range(LAYERS - 1, -1, -1):
        pre_act = pres[layer]
        sigmoid_z = jax.nn.sigmoid(pre_act)
        delta_low = (grad_h * sigmoid_z * (1.0 + pre_act * (1.0 - sigmoid_z))).astype(jnp.bfloat16)
        delta_sides[layer] = jnp.einsum(
            "esc,cr->esr", delta_low, proj_delta[assign[layer]], preferred_element_type=jnp.float32
        )
        input_sides[layer] = jnp.einsum(
            "esk,kt->est", wides[layer], proj_input[assign[layer]], preferred_element_type=jnp.float32
        )
        if layer > 0:
            back_wide = jnp.einsum(
                "esc,kc->esk", delta_low, conv_w[layer], preferred_element_type=jnp.float32
            )
            width = grad_h.shape[2]
            first_third = back_wide[:, :, :width]
            last_third = back_wide[:, :, 2 * width :]
            blank = jnp.zeros_like(first_third[:, :1])
            grad_input = back_wide[:, :, width : 2 * width]
            grad_input = grad_input + jnp.concatenate([first_third[:, 1:], blank], 1)
            grad_input = grad_input + jnp.concatenate([blank, last_third[:, :-1]], 1)
            grad_h = grad_h + grad_input
    layer_ids = jnp.arange(LAYERS, dtype=jnp.int32)
    same_before = jnp.sum(
        (assign[None, :] == assign[:, None]) & (layer_ids[None, :] < layer_ids[:, None]), axis=1
    )
    slot = assign * (LAYERS // blocks_here) + same_before
    order = jnp.sum(
        jnp.where(slot[None, :] == layer_ids[:, None], layer_ids[None, :], 0), axis=1
    )
    delta_stack = jnp.stack(delta_sides)[order]
    input_stack = jnp.stack(input_sides)[order]
    per_block = LAYERS // blocks_here
    delta_stack = delta_stack.reshape(blocks_here, per_block, examples, SEQ, PR)
    input_stack = input_stack.reshape(blocks_here, per_block, examples, SEQ, PS)
    panel = jnp.einsum(
        "bjesr,bjest->ebrt", delta_stack, input_stack, precision=lax.Precision.HIGH
    )
    return panel.reshape(examples, blocks_here * PR * PS).astype(jnp.bfloat16)


def on_device(left_feat, right_feat, embed, conv_w, head, assign, proj_delta, proj_input):
    group = ("zh", "core", "col")
    n_group = lax.axis_size(group)
    n_zh = lax.axis_size("zh")
    n_core = lax.axis_size("core")
    n_col = lax.axis_size("col")
    n_y = lax.axis_size("y")
    n_blk = lax.axis_size("pblk")
    left_each = left_feat.shape[0]
    right_each = right_feat.shape[2]
    right_local = right_feat.reshape(right_each, right_feat.shape[3])
    own_features = jnp.concatenate([left_feat, right_local], 0)
    panel = panels(own_features, embed, conv_w, head, assign, proj_delta, proj_input)
    own = panel.shape[0]
    width = panel.shape[1] // n_group
    sliced = panel.reshape(own, n_group, width)
    left_part = lax.all_to_all(sliced[:left_each], group, split_axis=1, concat_axis=0, tiled=True)
    left_part = left_part.reshape(n_group * left_each, width)
    left_tile = lax.all_gather(left_part, "pblk", axis=0, tiled=True)
    left_part, right_sliced = lax.optimization_barrier((left_part, sliced[left_each:]))
    right_part = lax.all_to_all(right_sliced, group, split_axis=1, concat_axis=0, tiled=True)
    right_part = right_part.reshape(n_group * right_each, width)
    up = [(j, (j + 1) % n_y) for j in range(n_y)]
    down = [(j, (j - 1) % n_y) for j in range(n_y)]
    from_below = lax.ppermute(right_part, "y", up)
    from_above = lax.ppermute(right_part, "y", down)
    half = right_part.shape[0] // 2
    far_low = lax.ppermute(from_below[:half], "y", up)
    far_high = lax.ppermute(from_above[half:], "y", down)
    far = jnp.concatenate([far_low, far_high], 0)
    right_tile = jnp.stack([far, from_below, right_part, from_above])
    left_tile = left_tile.reshape(n_blk, n_zh * n_core, n_col, left_each, width)
    left_tile = jnp.transpose(left_tile, (1, 2, 0, 3, 4)).reshape(-1, width)
    right_tile = right_tile.reshape(n_y, n_zh, n_core, n_col, right_each, width)
    right_tile = jnp.transpose(right_tile, (3, 1, 0, 2, 4, 5)).reshape(-1, width)
    partial_t = jnp.einsum("rk,lk->rl", right_tile, left_tile, preferred_element_type=jnp.float32)
    chunks = partial_t.reshape(n_col, partial_t.shape[0] // n_col, n_zh * n_core, -1)
    chunks = jnp.transpose(chunks, (2, 0, 1, 3)).reshape(n_group, chunks.shape[1], chunks.shape[3])
    chunks = chunks.reshape(n_zh, n_core, n_col, chunks.shape[1], chunks.shape[2])
    mine = lax.axis_index("core")
    swap = [(j, (j + 1) % n_core) for j in range(n_core)]
    for_partner = lax.dynamic_index_in_dim(chunks, 1 - mine, axis=1, keepdims=False)
    kept = lax.dynamic_index_in_dim(chunks, mine, axis=1, keepdims=False)
    paired = kept + lax.ppermute(for_partner, "core", swap)
    paired = paired.reshape(n_zh * n_col, paired.shape[2], paired.shape[3])
    received = lax.all_to_all(paired, ("zh", "col"), split_axis=0, concat_axis=0, tiled=True)
    block = jnp.sum(received, axis=0).T
    block = block.reshape(block.shape[0], n_zh, n_y, n_core * right_each)
    block = jnp.roll(block, lax.axis_index("y") - 2, axis=2)
    return block.reshape(block.shape[0], -1)


def solution(mesh):
    n_row = mesh.shape["row"]
    fine = Mesh(
        mesh.devices.reshape(2, 4, n_row // 8, mesh.shape["col"], mesh.shape["pblk"]),
        ("zh", "y", "core", "col", "pblk"),
    )
    rows = ("zh", "y", "core")
    placed = (
        P((*rows, "col", "pblk"), None),
        P("col", "pblk", rows, None),
        P(),
        P(),
        P(),
        P(),
        P(),
        P(),
    )
    return jax.shard_map(
        on_device, mesh=fine, in_specs=placed, out_specs=P(rows, ("col", "pblk")), check_vma=False
    )
```

```python
import jax
import jax.numpy as jnp
from jax import lax
from jax.sharding import Mesh, PartitionSpec as P

SEQ = 64
NFEAT = 4
VOCAB = 256
LAYERS = 8
PR = 128
PS = 128


def shift_wide(inputs):
    blank = jnp.zeros_like(inputs[:, :1])
    earlier = jnp.concatenate([blank, inputs[:, :-1]], 1)
    later_cells = jnp.concatenate([inputs[:, 1:], blank], 1)
    return jnp.concatenate([earlier, inputs, later_cells], 2)


def panels(features, embed, conv_w, head, assign, proj_delta, proj_input):
    examples = features.shape[0]
    blocks_here = proj_delta.shape[0]
    offsets = jnp.arange(NFEAT, dtype=jnp.int32) * VOCAB
    table_rows = features.reshape(examples, SEQ, NFEAT) + offsets
    table_ids = jnp.arange(NFEAT * VOCAB, dtype=jnp.int32)
    onehot = (table_rows[:, :, 0:1] == table_ids).astype(jnp.bfloat16)
    for field in range(1, NFEAT):
        onehot = onehot + (table_rows[:, :, field : field + 1] == table_ids).astype(jnp.bfloat16)
    hidden = jnp.einsum("esv,vc->esc", onehot, embed, preferred_element_type=jnp.float32)
    wides = []
    pres = []
    for layer in range(LAYERS):
        wide_input = shift_wide(hidden.astype(jnp.bfloat16))
        pre_act = jnp.einsum(
            "esk,kc->esc", wide_input, conv_w[layer], preferred_element_type=jnp.float32
        )
        wides.append(wide_input)
        pres.append(pre_act)
        hidden = hidden + jax.nn.silu(pre_act)
    grad_h = jnp.broadcast_to(head / SEQ, hidden.shape)
    delta_sides = [None] * LAYERS
    input_sides = [None] * LAYERS
    for layer in range(LAYERS - 1, -1, -1):
        pre_act = pres[layer]
        sigmoid_z = jax.nn.sigmoid(pre_act)
        delta_low = (grad_h * sigmoid_z * (1.0 + pre_act * (1.0 - sigmoid_z))).astype(jnp.bfloat16)
        delta_sides[layer] = jnp.einsum(
            "esc,cr->esr", delta_low, proj_delta[assign[layer]], preferred_element_type=jnp.float32
        )
        input_sides[layer] = jnp.einsum(
            "esk,kt->est", wides[layer], proj_input[assign[layer]], preferred_element_type=jnp.float32
        )
        if layer > 0:
            back_wide = jnp.einsum(
                "esc,kc->esk", delta_low, conv_w[layer], preferred_element_type=jnp.float32
            )
            width = grad_h.shape[2]
            first_third = back_wide[:, :, :width]
            last_third = back_wide[:, :, 2 * width :]
            blank = jnp.zeros_like(first_third[:, :1])
            grad_input = back_wide[:, :, width : 2 * width]
            grad_input = grad_input + jnp.concatenate([first_third[:, 1:], blank], 1)
            grad_input = grad_input + jnp.concatenate([blank, last_third[:, :-1]], 1)
            grad_h = grad_h + grad_input
    layer_ids = jnp.arange(LAYERS, dtype=jnp.int32)
    same_before = jnp.sum(
        (assign[None, :] == assign[:, None]) & (layer_ids[None, :] < layer_ids[:, None]), axis=1
    )
    slot = assign * (LAYERS // blocks_here) + same_before
    order = jnp.sum(
        jnp.where(slot[None, :] == layer_ids[:, None], layer_ids[None, :], 0), axis=1
    )
    delta_stack = jnp.zeros((LAYERS,) + delta_sides[0].shape, jnp.float32)
    input_stack = jnp.zeros((LAYERS,) + input_sides[0].shape, jnp.float32)
    for layer in range(LAYERS):
        delta_stack = lax.dynamic_update_index_in_dim(delta_stack, delta_sides[layer], slot[layer], 0)
        input_stack = lax.dynamic_update_index_in_dim(input_stack, input_sides[layer], slot[layer], 0)
    per_block = LAYERS // blocks_here
    delta_stack = delta_stack.reshape(blocks_here, per_block, examples, SEQ, PR)
    input_stack = input_stack.reshape(blocks_here, per_block, examples, SEQ, PS)
    panel = jnp.einsum(
        "bjesr,bjest->ebrt", delta_stack, input_stack, precision=lax.Precision.HIGH
    )
    return panel.reshape(examples, blocks_here * PR * PS).astype(jnp.bfloat16)


def on_device(left_feat, right_feat, embed, conv_w, head, assign, proj_delta, proj_input):
    group = ("zh", "core", "col")
    n_group = lax.axis_size(group)
    n_zh = lax.axis_size("zh")
    n_core = lax.axis_size("core")
    n_col = lax.axis_size("col")
    n_y = lax.axis_size("y")
    n_blk = lax.axis_size("pblk")
    left_each = left_feat.shape[0]
    right_each = right_feat.shape[2]
    right_local = right_feat.reshape(right_each, right_feat.shape[3])
    own_features = jnp.concatenate([left_feat, right_local], 0)
    panel = panels(own_features, embed, conv_w, head, assign, proj_delta, proj_input)
    own = panel.shape[0]
    width = panel.shape[1] // n_group
    sliced = panel.reshape(own, n_group, width)
    left_part = lax.all_to_all(sliced[:left_each], group, split_axis=1, concat_axis=0, tiled=True)
    left_part = left_part.reshape(n_group * left_each, width)
    left_tile = lax.all_gather(left_part, "pblk", axis=0, tiled=True)
    left_part, right_sliced = lax.optimization_barrier((left_part, sliced[left_each:]))
    right_part = lax.all_to_all(right_sliced, group, split_axis=1, concat_axis=0, tiled=True)
    right_part = right_part.reshape(n_group * right_each, width)
    up = [(j, (j + 1) % n_y) for j in range(n_y)]
    down = [(j, (j - 1) % n_y) for j in range(n_y)]
    from_below = lax.ppermute(right_part, "y", up)
    from_above = lax.ppermute(right_part, "y", down)
    half = right_part.shape[0] // 2
    far_low = lax.ppermute(from_below[:half], "y", up)
    far_high = lax.ppermute(from_above[half:], "y", down)
    far = jnp.concatenate([far_low, far_high], 0)
    right_tile = jnp.stack([far, from_below, right_part, from_above])
    left_tile = left_tile.reshape(n_blk, n_zh * n_core, n_col, left_each, width)
    left_tile = jnp.transpose(left_tile, (1, 2, 0, 3, 4)).reshape(-1, width)
    right_tile = right_tile.reshape(n_y, n_zh, n_core, n_col, right_each, width)
    right_tile = jnp.transpose(right_tile, (3, 1, 0, 2, 4, 5)).reshape(-1, width)
    partial_t = jnp.einsum("rk,lk->rl", right_tile, left_tile, preferred_element_type=jnp.float32)
    chunks = partial_t.reshape(n_col, partial_t.shape[0] // n_col, n_zh * n_core, -1)
    chunks = jnp.transpose(chunks, (2, 0, 1, 3)).reshape(n_group, chunks.shape[1], chunks.shape[3])
    chunks = chunks.reshape(n_zh, n_core, n_col, chunks.shape[1], chunks.shape[2])
    mine = lax.axis_index("core")
    swap = [(j, (j + 1) % n_core) for j in range(n_core)]
    for_partner = lax.dynamic_index_in_dim(chunks, 1 - mine, axis=1, keepdims=False)
    kept = lax.dynamic_index_in_dim(chunks, mine, axis=1, keepdims=False)
    paired = kept + lax.ppermute(for_partner, "core", swap)
    paired = paired.reshape(n_zh * n_col, paired.shape[2], paired.shape[3])
    received = lax.all_to_all(paired, ("zh", "col"), split_axis=0, concat_axis=0, tiled=True)
    block = jnp.sum(received, axis=0).T
    block = block.reshape(block.shape[0], n_zh, n_y, n_core * right_each)
    block = jnp.roll(block, lax.axis_index("y") - 2, axis=2)
    return block.reshape(block.shape[0], -1)


def solution(mesh):
    n_row = mesh.shape["row"]
    fine = Mesh(
        mesh.devices.reshape(2, 4, n_row // 8, mesh.shape["col"], mesh.shape["pblk"]),
        ("zh", "y", "core", "col", "pblk"),
    )
    rows = ("zh", "y", "core")
    placed = (
        P((*rows, "col", "pblk"), None),
        P("col", "pblk", rows, None),
        P(),
        P(),
        P(),
        P(),
        P(),
        P(),
    )
    return jax.shard_map(
        on_device, mesh=fine, in_specs=placed, out_specs=P(rows, ("col", "pblk")), check_vma=False
    )
```
